256 devices in a mesh: band: 16 (over x, y_hi, core), req: 16 (over y_lo, z).
Axes of the slice: x: 4, y: 4 (y_hi: 2, y_lo: 2; y = y_hi * 2 + y_lo), z: 8, core: 2. Of those that a mesh axis runs over, the one named last changes fastest.
Arguments:
- latents: bfloat16 [16, 64, 512, 320], P('req', 'band'), may hold values from -40 to 40
- request_time_embedding: bfloat16 [16, 1280], P('req'), may hold values from -6 to 6
- request_adapter: int32 [16, 1], P('req'), may hold values from 0 to 255, as said below
- adapter_stored_row: int32 [256], replicated, may hold values from 0 to 255, as said below
- first_conv_weight: bfloat16 [3, 3, 320, 320], replicated, may hold values from -0.109375 to 0.109375
- stored_down_weight: bfloat16 [256, 3, 3, 320, 64], P(('band', 'req')), may hold values from -0.109375 to 0.109375
- stored_up_weight: bfloat16 [256, 64, 320], P(('band', 'req')), may hold values from -0.75 to 0.75
- second_conv_weight: bfloat16 [3, 3, 320, 320], replicated, may hold values from -0.109375 to 0.109375
- time_projection_weight: bfloat16 [1280, 320], replicated, may hold values from -0.15625 to 0.15625
Outputs:
- block_out: bfloat16 [16, 64, 512, 320], P('req', 'band')
The draws below stay inside these ranges and needn't reach their ends.
Inputs may be any that keep to these rules, and one draw needn't show every extreme that they name: `request_adapter`: ids of adapters. `adapter_stored_row`: each stored row appears once.
All inputs are finite; a program needn't handle non-finite values.
Results may differ from the reference program's by a relative error of at most 0.0038.
Values may be sent and summed in bfloat16 or wider, within the bound.
No kernel may reach another device: no remote copies, remote signals or barrier semaphores. Data moves between devices by JAX's collectives and lax.ppermute only.
A program may use at most 128 MiB of HBM per device.

```python
import jax
import jax.numpy as jnp
from jax import lax

CHANNEL_COUNT = 320
G = 32
TD = 1280
ADAPTER_RANK = 64
W = 512
ADAPT_DEV = 1
REQ_DEV = 1
H = 64
REQUESTS = 16
ADAPTER_TOTAL = 256


def draw_latents(key, part):
    key_base = jax.random.fold_in(key, 11)
    key_chan = jax.random.fold_in(key, 12)
    base = jnp.clip(jax.random.normal(key_base, (REQUESTS, H, W, CHANNEL_COUNT), jnp.float32), -6.0, 6.0)
    position = jnp.arange(H, dtype=jnp.float32) / max(H - 1, 1)
    row_scale = 0.5 + position
    chan_scale = jnp.exp(jax.random.uniform(key_chan, (CHANNEL_COUNT,), jnp.float32, jnp.log(0.5), jnp.log(2.0)))
    values = base * row_scale[None, :, None, None] * chan_scale[None, None, None, :]
    return values.astype(jnp.bfloat16)


def stored_order(key):
    return jax.random.permutation(jax.random.fold_in(key, 7), ADAPTER_TOTAL).astype(jnp.int32)


def draw_adapter_stored_row(key, part):
    return stored_order(key)


def draw_request_adapter(key, part):
    order = stored_order(key)
    inverse = jnp.argsort(order).astype(jnp.int32)
    req_count = REQUESTS // REQ_DEV
    band_count = ADAPTER_TOTAL // (ADAPT_DEV * req_count)
    request_ids = jnp.arange(REQUESTS, dtype=jnp.int32)
    own_req = request_ids // REQ_DEV
    random_req = jax.random.randint(jax.random.fold_in(key, 21), (REQUESTS,), 0, req_count, jnp.int32)
    far_req = (own_req + req_count // 2) % req_count
    target_req = jnp.where(request_ids % 2 == 0, far_req, random_req)
    target_band = jax.random.randint(jax.random.fold_in(key, 22), (REQUESTS,), 0, band_count, jnp.int32)
    local_slot = jax.random.randint(jax.random.fold_in(key, 23), (REQUESTS,), 0, ADAPT_DEV, jnp.int32)
    stored = (target_band * req_count + target_req) * ADAPT_DEV + local_slot
    ids = inverse[stored]
    ids = jnp.where(request_ids == 0, jnp.int32(ADAPTER_TOTAL - 1), ids)
    ids = jnp.where(request_ids == 1, jnp.int32(0), ids)
    return ids.astype(jnp.int32).reshape(REQUESTS, 1)


def shard_levels(stream_key, shape, split, low, high):
    gain = 1.0
    for dim, shards_of in split:
        steps = jax.random.uniform(jax.random.fold_in(jax.random.fold_in(stream_key, 6), dim), (shards_of,), jnp.float32, low / len(split), high / len(split))
        gain = gain * jnp.repeat(jnp.exp(steps), shape[dim] // shards_of).reshape((-1,) + (1,) * (len(shape) - 1 - dim))
    return gain


def scatter_about(key, dims, width, limit, shards=(), kind=jnp.bfloat16):
    values = jax.random.normal(key, dims, jnp.float32) * width
    if len(shards) > 0:
        values = shard_levels(key, dims, shards, -0.22, 0.18) * values
    return jnp.clip(values, min=-limit, max=limit).astype(kind)


def setup_inputs(seed: int = 0) -> dict:
    key_list = jax.random.split(jax.random.key(seed), 10)
    latents = draw_latents(jax.random.fold_in(key_list[9], 71), 0)
    request_time_embedding = scatter_about(key_list[1], (REQUESTS, TD), 1.0, 6.0, ((0, 16),))
    request_adapter = draw_request_adapter(jax.random.fold_in(key_list[9], 71), 0)
    adapter_stored_row = draw_adapter_stored_row(jax.random.fold_in(key_list[9], 71), 0)
    first_conv_weight = scatter_about(key_list[4], (3, 3, CHANNEL_COUNT, CHANNEL_COUNT), (9 * CHANNEL_COUNT) ** -0.5, 0.109375)
    stored_down_weight = scatter_about(key_list[5], (ADAPTER_TOTAL, 3, 3, CHANNEL_COUNT, ADAPTER_RANK), (9 * CHANNEL_COUNT) ** -0.5, 0.109375, ((0, 256),))
    stored_up_weight = scatter_about(key_list[6], (ADAPTER_TOTAL, ADAPTER_RANK, CHANNEL_COUNT), ADAPTER_RANK ** -0.5, 0.75, ((0, 256),))
    second_conv_weight = scatter_about(key_list[7], (3, 3, CHANNEL_COUNT, CHANNEL_COUNT), (9 * CHANNEL_COUNT) ** -0.5, 0.109375)
    time_projection_weight = scatter_about(key_list[8], (TD, CHANNEL_COUNT), TD ** -0.5, 0.15625)
    return {"latents": latents, "request_time_embedding": request_time_embedding, "request_adapter": request_adapter, "adapter_stored_row": adapter_stored_row, "first_conv_weight": first_conv_weight, "stored_down_weight": stored_down_weight, "stored_up_weight": stored_up_weight, "second_conv_weight": second_conv_weight, "time_projection_weight": time_projection_weight}


def group_norm(field):
    grouped = field.reshape(H, W, G, CHANNEL_COUNT // G)
    center = lax.optimization_barrier(jnp.mean(grouped, axis=(0, 1, 3), keepdims=True))
    spread = lax.optimization_barrier(jnp.mean((grouped - center) ** 2, axis=(0, 1, 3), keepdims=True))
    return ((grouped - center) * lax.rsqrt(spread + 1e-05)).reshape(H, W, CHANNEL_COUNT)

def convolve(padded, kernel):
    total = None
    for row_tap in range(3):
        for col_tap in range(3):
            term = jnp.einsum('hwc,cd->hwd', padded[row_tap:row_tap + H, col_tap:col_tap + W], kernel[row_tap, col_tap].astype(jnp.float32))
            total = term if total is None else total + term
    return total

def pad_field(field):
    return jnp.pad(field.astype(jnp.float32), ((1, 1), (1, 1), (0, 0)))

def reference(latents, request_time_embedding, request_adapter, adapter_stored_row, first_conv_weight, stored_down_weight, stored_up_weight, second_conv_weight, time_projection_weight):
    shifts = jnp.dot(jax.nn.silu(request_time_embedding.astype(jnp.float32)).astype(jnp.bfloat16), time_projection_weight, preferred_element_type=jnp.float32)

    def one_request(items):
        image, chosen, shift = items
        stored_index = adapter_stored_row[chosen[0]]
        down_matrix = lax.dynamic_index_in_dim(stored_down_weight, stored_index, 0, keepdims=False)
        up_matrix = lax.dynamic_index_in_dim(stored_up_weight, stored_index, 0, keepdims=False)
        first = jax.nn.silu(group_norm(image.astype(jnp.float32))).astype(jnp.bfloat16)
        padded = pad_field(first)
        main = convolve(padded, first_conv_weight)
        lowrank = convolve(padded, down_matrix).astype(jnp.bfloat16)
        lifted = jnp.dot(lowrank.reshape(H * W, ADAPTER_RANK), up_matrix, preferred_element_type=jnp.float32).reshape(H, W, CHANNEL_COUNT)
        hidden = main + lifted + shift[None, None, :]
        second = jax.nn.silu(group_norm(hidden)).astype(jnp.bfloat16)
        result = image.astype(jnp.float32) + convolve(pad_field(second), second_conv_weight)
        return result.astype(jnp.bfloat16)
    return lax.map(one_request, (latents, request_adapter, shifts))
```

```python
import jax
import jax.numpy as jnp
from jax import lax
from jax.sharding import PartitionSpec as P

G = 32


def with_halo(x, sides, width):
    for axis, dim in sides:
        count, length = (lax.axis_size(axis), x.shape[dim])
        up = [(i, (i + 1) % count) for i in range(count - 1)]
        down = [(j, i) for i, j in up]
        last = lax.slice_in_dim(x, length - width, length, axis=dim)
        initial = lax.slice_in_dim(x, 0, width, axis=dim)
        before = lax.ppermute(last, axis, up)
        after = lax.ppermute(initial, axis, down)
        x = jnp.concatenate([before, x, after], axis=dim)
    return x


def exchange(value, axis):
    count = lax.axis_size(axis)
    spread = jnp.broadcast_to(value[None], (count,) + value.shape)
    return lax.all_to_all(spread, axis, 0, 0, tiled=True)


def group_norm(field, groups):
    requests, rows, width, channels = field.shape
    grouped = field.reshape(requests, rows, width, groups, channels // groups)
    count = rows * width * (channels // groups)
    local_mean = jnp.sum(grouped, axis=(1, 2, 4)) / count
    deviation = grouped - local_mean[:, None, None, :, None]
    local_m2 = jnp.sum(deviation * deviation, axis=(1, 2, 4))
    stats = exchange(jnp.stack([local_mean, local_m2]), "band")
    means, m2s = stats[:, 0], stats[:, 1]
    bands = means.shape[0]
    mean = jnp.sum(means, axis=0) / bands
    gap = means - mean[None]
    m2 = jnp.sum(m2s, axis=0) + count * jnp.sum(gap * gap, axis=0)
    spread = m2 / (count * bands)
    centered = grouped - mean[:, None, None, :, None]
    normed = centered * lax.rsqrt(spread + 1e-05)[:, None, None, :, None]
    return normed.reshape(field.shape)


def padded_field(field):
    extended = with_halo(field, (("band", 1),), 1)
    return jnp.pad(extended, ((0, 0), (0, 0), (1, 1), (0, 0)))


def convolve(padded, kernel, rows, width):
    total = None
    for row_tap in range(3):
        for col_tap in range(3):
            term = jnp.einsum(
                "qhwc,cd->qhwd",
                padded[:, row_tap : row_tap + rows, col_tap : col_tap + width],
                kernel[row_tap, col_tap],
                preferred_element_type=jnp.float32,
            )
            total = term if total is None else total + term
    return total


def fetch_adapter(slots, down, up):
    bands, reqs = lax.axis_size("band"), lax.axis_size("req")
    flat = jnp.concatenate([down.reshape(-1), up.reshape(-1)])
    pieces = flat.reshape(bands, -1)
    by_band = lax.all_to_all(pieces, "band", 0, 0, tiled=True)
    wanted = jnp.take(by_band, slots // reqs, axis=0)
    by_req = lax.all_to_all(wanted, "req", 0, 0, tiled=True)
    own = lax.axis_index("req")
    mine = lax.dynamic_index_in_dim(by_req, slots[own] % reqs, 0, keepdims=True)
    whole = lax.all_gather(mine, "band", axis=0, tiled=True).reshape(-1)
    down_size = down.size
    return whole[:down_size].reshape(down.shape[1:]), whole[down_size:].reshape(up.shape[1:])


def shards(
    latents,
    request_time_embedding,
    request_adapter,
    adapter_stored_row,
    first_conv_weight,
    stored_down_weight,
    stored_up_weight,
    second_conv_weight,
    time_projection_weight,
):
    requests, rows, width, channels = latents.shape
    slots = jnp.take(adapter_stored_row, request_adapter[:, 0], axis=0)
    chosen_down, chosen_up = fetch_adapter(slots, stored_down_weight, stored_up_weight)
    shift = jnp.dot(
        jax.nn.silu(request_time_embedding.astype(jnp.float32)).astype(jnp.bfloat16),
        time_projection_weight,
        preferred_element_type=jnp.float32,
    )
    first = jax.nn.silu(group_norm(latents.astype(jnp.float32), G)).astype(jnp.bfloat16)
    first_padded = padded_field(first)
    main = convolve(first_padded, first_conv_weight, rows, width)
    lowrank = convolve(first_padded, chosen_down, rows, width).astype(jnp.bfloat16)
    lifted = jnp.einsum("qhwk,kc->qhwc", lowrank, chosen_up, preferred_element_type=jnp.float32)
    hidden = main + lifted + shift[:, None, None, :]
    second = jax.nn.silu(group_norm(hidden, G)).astype(jnp.bfloat16)
    result = latents.astype(jnp.float32) + convolve(
        padded_field(second), second_conv_weight, rows, width
    )
    return result.astype(jnp.bfloat16)


def solution(mesh):
    in_specs = (
        P("req", "band", None, None),
        P("req", None),
        P(),
        P(),
        P(),
        P(("band", "req"), None, None, None, None),
        P(("band", "req"), None, None),
        P(),
        P(),
    )
    out_specs = P("req", "band", None, None)
    return jax.shard_map(shards, mesh=mesh, in_specs=in_specs, out_specs=out_specs, check_vma=False)
```

```python
import jax
import jax.numpy as jnp
from jax import lax
from jax.sharding import PartitionSpec as P

G = 32


def with_halo(x, sides, width):
    for axis, dim in sides:
        count, length = (lax.axis_size(axis), x.shape[dim])
        up = [(i, (i + 1) % count) for i in range(count - 1)]
        down = [(j, i) for i, j in up]
        last = lax.slice_in_dim(x, length - width, length, axis=dim)
        initial = lax.slice_in_dim(x, 0, width, axis=dim)
        before = lax.ppermute(last, axis, up)
        after = lax.ppermute(initial, axis, down)
        x = jnp.concatenate([before, x, after], axis=dim)
    return x


def exchange(value, axis):
    count = lax.axis_size(axis)
    spread = jnp.broadcast_to(value[None], (count,) + value.shape)
    return lax.all_to_all(spread, axis, 0, 0, tiled=True)


def group_norm(field, groups):
    requests, rows, width, channels = field.shape
    grouped = field.reshape(requests, rows, width, groups, channels // groups)
    count = rows * width * (channels // groups)
    local_mean = jnp.sum(grouped, axis=(1, 2, 4)) / count
    deviation = grouped - local_mean[:, None, None, :, None]
    local_m2 = jnp.sum(deviation * deviation, axis=(1, 2, 4))
    stats = exchange(jnp.stack([local_mean, local_m2]), "band")
    means, m2s = stats[:, 0], stats[:, 1]
    bands = means.shape[0]
    mean = jnp.sum(means, axis=0) / bands
    gap = means - mean[None]
    m2 = jnp.sum(m2s, axis=0) + count * jnp.sum(gap * gap, axis=0)
    spread = m2 / (count * bands)
    centered = grouped - mean[:, None, None, :, None]
    normed = centered * lax.rsqrt(spread + 1e-05)[:, None, None, :, None]
    return normed.reshape(field.shape)


def padded_field(field):
    extended = with_halo(field, (("band", 1),), 1)
    return jnp.pad(extended, ((0, 0), (0, 0), (1, 1), (0, 0)))


def convolve(padded, kernel):
    return lax.conv_general_dilated(
        padded,
        kernel,
        window_strides=(1, 1),
        padding="VALID",
        dimension_numbers=("NHWC", "HWIO", "NHWC"),
        preferred_element_type=jnp.float32,
    )


def fetch_adapter(slots, down, up):
    bands, reqs = lax.axis_size("band"), lax.axis_size("req")
    flat = jnp.concatenate([down.reshape(-1), up.reshape(-1)])
    pieces = flat.reshape(bands, -1)
    by_band = lax.all_to_all(pieces, "band", 0, 0, tiled=True)
    wanted = jnp.take(by_band, slots // reqs, axis=0)
    by_req = lax.all_to_all(wanted, "req", 0, 0, tiled=True)
    own = lax.axis_index("req")
    mine = lax.dynamic_index_in_dim(by_req, slots[own] % reqs, 0, keepdims=True)
    whole = exchange(mine[0], "band").reshape(-1)
    down_size = down.size
    return whole[:down_size].reshape(down.shape[1:]), whole[down_size:].reshape(up.shape[1:])


def shards(
    latents,
    request_time_embedding,
    request_adapter,
    adapter_stored_row,
    first_conv_weight,
    stored_down_weight,
    stored_up_weight,
    second_conv_weight,
    time_projection_weight,
):
    requests, rows, width, channels = latents.shape
    every_adapter = exchange(request_adapter[0, 0], "req")
    slots = jnp.take(adapter_stored_row, every_adapter, axis=0)
    chosen_down, chosen_up = fetch_adapter(slots, stored_down_weight, stored_up_weight)
    shift = jnp.dot(
        jax.nn.silu(request_time_embedding.astype(jnp.float32)).astype(jnp.bfloat16),
        time_projection_weight,
        preferred_element_type=jnp.float32,
    )
    first = jax.nn.silu(group_norm(latents.astype(jnp.float32), G)).astype(jnp.bfloat16)
    first_padded = padded_field(first)
    both = convolve(first_padded, jnp.concatenate([first_conv_weight, chosen_down], axis=3))
    main = both[..., :channels]
    lowrank = both[..., channels:].astype(jnp.bfloat16)
    lifted = jnp.einsum("qhwk,kc->qhwc", lowrank, chosen_up, preferred_element_type=jnp.float32)
    hidden = main + lifted + shift[:, None, None, :]
    second = jax.nn.silu(group_norm(hidden, G)).astype(jnp.bfloat16)
    result = latents.astype(jnp.float32) + convolve(padded_field(second), second_conv_weight)
    return result.astype(jnp.bfloat16)


def solution(mesh):
    in_specs = (
        P("req", "band", None, None),
        P("req", None),
        P("req", None),
        P(),
        P(),
        P(("band", "req"), None, None, None, None),
        P(("band", "req"), None, None),
        P(),
        P(),
    )
    out_specs = P("req", "band", None, None)
    return jax.shard_map(shards, mesh=mesh, in_specs=in_specs, out_specs=out_specs, check_vma=False)
```

```python
import jax
import jax.numpy as jnp
from jax import lax
from jax.experimental import pallas as pl
from jax.sharding import PartitionSpec as P

G = 32


def with_halo(x, sides, width):
    for axis, dim in sides:
        count, length = (lax.axis_size(axis), x.shape[dim])
        up = [(i, (i + 1) % count) for i in range(count - 1)]
        down = [(j, i) for i, j in up]
        last = lax.slice_in_dim(x, length - width, length, axis=dim)
        initial = lax.slice_in_dim(x, 0, width, axis=dim)
        before = lax.ppermute(last, axis, up)
        after = lax.ppermute(initial, axis, down)
        x = jnp.concatenate([before, x, after], axis=dim)
    return x


def exchange(value, axis):
    count = lax.axis_size(axis)
    spread = jnp.broadcast_to(value[None], (count,) + value.shape)
    return lax.all_to_all(spread, axis, 0, 0, tiled=True)


def group_norm(field, groups):
    requests, rows, width, channels = field.shape
    grouped = field.reshape(requests, rows, width, groups, channels // groups)
    count = rows * width * (channels // groups)
    local_mean = jnp.sum(grouped, axis=(1, 2, 4)) / count
    deviation = grouped - local_mean[:, None, None, :, None]
    local_m2 = jnp.sum(deviation * deviation, axis=(1, 2, 4))
    stats = exchange(jnp.stack([local_mean, local_m2]), "band")
    means, m2s = stats[:, 0], stats[:, 1]
    bands = means.shape[0]
    mean = jnp.sum(means, axis=0) / bands
    gap = means - mean[None]
    m2 = jnp.sum(m2s, axis=0) + count * jnp.sum(gap * gap, axis=0)
    spread = m2 / (count * bands)
    centered = grouped - mean[:, None, None, :, None]
    normed = centered * lax.rsqrt(spread + 1e-05)[:, None, None, :, None]
    return normed.reshape(field.shape)


def padded_field(field):
    extended = with_halo(field, (("band", 1),), 1)
    return jnp.pad(extended, ((0, 0), (0, 0), (1, 1), (0, 0)))


def taps_by_column(padded):
    width = padded.shape[1] - 2
    return jnp.concatenate([padded[:, tap : tap + width] for tap in range(3)], axis=-1)


def first_conv_kernel(x_ref, w_ref, d_ref, u_ref, s_ref, o_ref):
    row = pl.program_id(0)
    main = None
    low = None
    for tap in range(3):
        piece = x_ref[row + tap]
        m = jnp.dot(piece, w_ref[tap], preferred_element_type=jnp.float32)
        l = jnp.dot(piece, d_ref[tap], preferred_element_type=jnp.float32)
        main = m if main is None else main + m
        low = l if low is None else low + l
    lifted = jnp.dot(low.astype(jnp.bfloat16), u_ref[...], preferred_element_type=jnp.float32)
    o_ref[0] = main + lifted + s_ref[...]


def second_conv_kernel(x_ref, w_ref, r_ref, o_ref):
    row = pl.program_id(0)
    total = None
    for tap in range(3):
        t = jnp.dot(x_ref[row + tap], w_ref[tap], preferred_element_type=jnp.float32)
        total = t if total is None else total + t
    o_ref[0] = (r_ref[0].astype(jnp.float32) + total).astype(o_ref.dtype)


def first_conv(cols, weight, down, up, shift):
    rows, width, wide = cols.shape[0] - 2, cols.shape[1], cols.shape[2]
    out = weight.shape[-1]
    rank = down.shape[-1]
    flops = 2 * rows * width * wide * (out + rank) + 2 * rows * width * rank * out
    return pl.pallas_call(
        first_conv_kernel,
        grid=(rows,),
        in_specs=[
            pl.BlockSpec(cols.shape, lambda h: (0, 0, 0)),
            pl.BlockSpec(weight.shape, lambda h: (0, 0, 0)),
            pl.BlockSpec(down.shape, lambda h: (0, 0, 0)),
            pl.BlockSpec(up.shape, lambda h: (0, 0)),
            pl.BlockSpec(shift.shape, lambda h: (0, 0)),
        ],
        out_specs=pl.BlockSpec((1, width, out), lambda h: (h, 0, 0)),
        out_shape=jax.ShapeDtypeStruct((rows, width, out), jnp.float32),
        cost_estimate=pl.CostEstimate(
            flops=flops, transcendentals=0,
            bytes_accessed=cols.size * 2 + weight.size * 2 + down.size * 2 + rows * width * out * 4,
        ),
    )(cols, weight, down, up, shift)


def second_conv(cols, weight, residual):
    rows, width, wide = cols.shape[0] - 2, cols.shape[1], cols.shape[2]
    out = weight.shape[-1]
    return pl.pallas_call(
        second_conv_kernel,
        grid=(rows,),
        in_specs=[
            pl.BlockSpec(cols.shape, lambda h: (0, 0, 0)),
            pl.BlockSpec(weight.shape, lambda h: (0, 0, 0)),
            pl.BlockSpec((1, width, out), lambda h: (h, 0, 0)),
        ],
        out_specs=pl.BlockSpec((1, width, out), lambda h: (h, 0, 0)),
        out_shape=jax.ShapeDtypeStruct((rows, width, out), residual.dtype),
        cost_estimate=pl.CostEstimate(
            flops=2 * rows * width * wide * out, transcendentals=0,
            bytes_accessed=cols.size * 2 + weight.size * 2 + rows * width * out * 4,
        ),
    )(cols, weight, residual)


def fetch_adapter(slots, down, up):
    bands, reqs = lax.axis_size("band"), lax.axis_size("req")
    flat = jnp.concatenate([down.reshape(-1), up.reshape(-1)])
    pieces = flat.reshape(bands, -1)
    by_band = lax.all_to_all(pieces, "band", 0, 0, tiled=True)
    wanted = jnp.take(by_band, slots // reqs, axis=0)
    by_req = lax.all_to_all(wanted, "req", 0, 0, tiled=True)
    own = lax.axis_index("req")
    mine = lax.dynamic_index_in_dim(by_req, slots[own] % reqs, 0, keepdims=True)
    whole = exchange(mine[0], "band").reshape(-1)
    down_size = down.size
    return whole[:down_size].reshape(down.shape[1:]), whole[down_size:].reshape(up.shape[1:])


def shards(
    latents,
    request_time_embedding,
    request_adapter,
    adapter_stored_row,
    first_conv_weight,
    stored_down_weight,
    stored_up_weight,
    second_conv_weight,
    time_projection_weight,
):
    requests, rows, width, channels = latents.shape
    every_adapter = exchange(request_adapter[0, 0], "req")
    slots = jnp.take(adapter_stored_row, every_adapter, axis=0)
    chosen_down, chosen_up = fetch_adapter(slots, stored_down_weight, stored_up_weight)
    shift = jnp.dot(
        jax.nn.silu(request_time_embedding.astype(jnp.float32)).astype(jnp.bfloat16),
        time_projection_weight,
        preferred_element_type=jnp.float32,
    )
    first = jax.nn.silu(group_norm(latents.astype(jnp.float32), G)).astype(jnp.bfloat16)
    wide = 3 * channels
    hidden = first_conv(
        taps_by_column(padded_field(first)[0]),
        first_conv_weight.reshape(3, wide, channels),
        chosen_down.reshape(3, wide, chosen_down.shape[-1]),
        chosen_up,
        shift,
    )[None]
    second = jax.nn.silu(group_norm(hidden, G)).astype(jnp.bfloat16)
    result = second_conv(
        taps_by_column(padded_field(second)[0]),
        second_conv_weight.reshape(3, wide, channels),
        latents[0],
    )
    return result[None]


def solution(mesh):
    in_specs = (
        P("req", "band", None, None),
        P("req", None),
        P("req", None),
        P(),
        P(),
        P(("band", "req"), None, None, None, None),
        P(("band", "req"), None, None),
        P(),
        P(),
    )
    out_specs = P("req", "band", None, None)
    return jax.shard_map(shards, mesh=mesh, in_specs=in_specs, out_specs=out_specs, check_vma=False)
```

```python
import jax
import jax.numpy as jnp
from jax import lax
from jax.experimental import pallas as pl
from jax.sharding import PartitionSpec as P

G = 32


def with_halo(x, sides, width):
    for axis, dim in sides:
        count, length = (lax.axis_size(axis), x.shape[dim])
        up = [(i, (i + 1) % count) for i in range(count - 1)]
        down = [(j, i) for i, j in up]
        last = lax.slice_in_dim(x, length - width, length, axis=dim)
        initial = lax.slice_in_dim(x, 0, width, axis=dim)
        before = lax.ppermute(last, axis, up)
        after = lax.ppermute(initial, axis, down)
        x = jnp.concatenate([before, x, after], axis=dim)
    return x


def exchange(value, axis):
    count = lax.axis_size(axis)
    spread = jnp.broadcast_to(value[None], (count,) + value.shape)
    return lax.all_to_all(spread, axis, 0, 0, tiled=True)


def group_norm(field, groups):
    requests, rows, width, channels = field.shape
    grouped = field.reshape(requests, rows, width, groups, channels // groups)
    count = rows * width * (channels // groups)
    local_mean = jnp.sum(grouped, axis=(1, 2, 4)) / count
    deviation = grouped - local_mean[:, None, None, :, None]
    local_m2 = jnp.sum(deviation * deviation, axis=(1, 2, 4))
    stats = exchange(jnp.stack([local_mean, local_m2]), "band")
    means, m2s = stats[:, 0], stats[:, 1]
    bands = means.shape[0]
    mean = jnp.sum(means, axis=0) / bands
    gap = means - mean[None]
    m2 = jnp.sum(m2s, axis=0) + count * jnp.sum(gap * gap, axis=0)
    spread = m2 / (count * bands)
    centered = grouped - mean[:, None, None, :, None]
    normed = centered * lax.rsqrt(spread + 1e-05)[:, None, None, :, None]
    return normed.reshape(field.shape)


def padded_field(field):
    extended = with_halo(field, (("band", 1),), 1)
    return jnp.pad(extended, ((0, 0), (0, 0), (1, 1), (0, 0)))


def taps_by_column(padded):
    width = padded.shape[1] - 2
    return jnp.concatenate([padded[:, tap : tap + width] for tap in range(3)], axis=-1)


def first_conv_kernel(x_ref, w_ref, d_ref, u_ref, s_ref, o_ref):
    row = pl.program_id(0)
    main = None
    low = None
    for tap in range(3):
        piece = x_ref[row + tap]
        m = jnp.dot(piece, w_ref[tap], preferred_element_type=jnp.float32)
        l = jnp.dot(piece, d_ref[tap], preferred_element_type=jnp.float32)
        main = m if main is None else main + m
        low = l if low is None else low + l
    lifted = jnp.dot(low.astype(jnp.bfloat16), u_ref[...], preferred_element_type=jnp.float32)
    o_ref[0] = main + lifted + s_ref[...]


def second_conv_kernel(x_ref, w_ref, r_ref, o_ref):
    row = pl.program_id(0)
    total = None
    for tap in range(3):
        t = jnp.dot(x_ref[row + tap], w_ref[tap], preferred_element_type=jnp.float32)
        total = t if total is None else total + t
    o_ref[0] = (r_ref[0].astype(jnp.float32) + total).astype(o_ref.dtype)


def first_conv(cols, weight, down, up, shift):
    rows, width, wide = cols.shape[0] - 2, cols.shape[1], cols.shape[2]
    out = weight.shape[-1]
    rank = down.shape[-1]
    flops = 2 * rows * width * wide * (out + rank) + 2 * rows * width * rank * out
    return pl.pallas_call(
        first_conv_kernel,
        grid=(rows,),
        in_specs=[
            pl.BlockSpec(cols.shape, lambda h: (0, 0, 0)),
            pl.BlockSpec(weight.shape, lambda h: (0, 0, 0)),
            pl.BlockSpec(down.shape, lambda h: (0, 0, 0)),
            pl.BlockSpec(up.shape, lambda h: (0, 0)),
            pl.BlockSpec(shift.shape, lambda h: (0, 0)),
        ],
        out_specs=pl.BlockSpec((1, width, out), lambda h: (h, 0, 0)),
        out_shape=jax.ShapeDtypeStruct((rows, width, out), jnp.float32),
        cost_estimate=pl.CostEstimate(
            flops=flops, transcendentals=0,
            bytes_accessed=cols.size * 2 + weight.size * 2 + down.size * 2 + rows * width * out * 4,
        ),
    )(cols, weight, down, up, shift)


def second_conv(cols, weight, residual):
    rows, width, wide = cols.shape[0] - 2, cols.shape[1], cols.shape[2]
    out = weight.shape[-1]
    return pl.pallas_call(
        second_conv_kernel,
        grid=(rows,),
        in_specs=[
            pl.BlockSpec(cols.shape, lambda h: (0, 0, 0)),
            pl.BlockSpec(weight.shape, lambda h: (0, 0, 0)),
            pl.BlockSpec((1, width, out), lambda h: (h, 0, 0)),
        ],
        out_specs=pl.BlockSpec((1, width, out), lambda h: (h, 0, 0)),
        out_shape=jax.ShapeDtypeStruct((rows, width, out), residual.dtype),
        cost_estimate=pl.CostEstimate(
            flops=2 * rows * width * wide * out, transcendentals=0,
            bytes_accessed=cols.size * 2 + weight.size * 2 + rows * width * out * 4,
        ),
    )(cols, weight, residual)


def fetch_adapter(slots, down, up):
    bands, reqs = lax.axis_size("band"), lax.axis_size("req")
    flat = jnp.concatenate([down.reshape(-1), up.reshape(-1)])
    lanes, sublanes = 128, 16
    piece_rows = -(-flat.size // (bands * lanes * sublanes)) * sublanes
    flat = jnp.pad(flat, (0, bands * piece_rows * lanes - flat.size))
    pieces = flat.reshape(bands, piece_rows, lanes)
    by_band = lax.all_to_all(pieces, "band", 0, 0, tiled=True)
    wanted = jnp.take(by_band, slots // reqs, axis=0)
    by_req = lax.all_to_all(wanted, "req", 0, 0, tiled=True)
    own = lax.axis_index("req")
    mine = lax.dynamic_index_in_dim(by_req, slots[own] % reqs, 0, keepdims=False)
    whole = exchange(mine, "band").reshape(-1)
    down_size = down.size
    chosen_down = whole[:down_size].reshape(down.shape[1:])
    chosen_up = whole[down_size : down_size + up.size].reshape(up.shape[1:])
    return chosen_down, chosen_up


def shards(
    latents,
    request_time_embedding,
    request_adapter,
    adapter_stored_row,
    first_conv_weight,
    stored_down_weight,
    stored_up_weight,
    second_conv_weight,
    time_projection_weight,
):
    requests, rows, width, channels = latents.shape
    every_adapter = exchange(request_adapter[0, 0], "req")
    slots = jnp.take(adapter_stored_row, every_adapter, axis=0)
    chosen_down, chosen_up = fetch_adapter(slots, stored_down_weight, stored_up_weight)
    shift = jnp.dot(
        jax.nn.silu(request_time_embedding.astype(jnp.float32)).astype(jnp.bfloat16),
        time_projection_weight,
        preferred_element_type=jnp.float32,
    )
    first = jax.nn.silu(group_norm(latents.astype(jnp.float32), G)).astype(jnp.bfloat16)
    wide = 3 * channels
    hidden = first_conv(
        taps_by_column(padded_field(first)[0]),
        first_conv_weight.reshape(3, wide, channels),
        chosen_down.reshape(3, wide, chosen_down.shape[-1]),
        chosen_up,
        shift,
    )[None]
    second = jax.nn.silu(group_norm(hidden, G)).astype(jnp.bfloat16)
    result = second_conv(
        taps_by_column(padded_field(second)[0]),
        second_conv_weight.reshape(3, wide, channels),
        latents[0],
    )
    return result[None]


def solution(mesh):
    in_specs = (
        P("req", "band", None, None),
        P("req", None),
        P("req", None),
        P(),
        P(),
        P(("band", "req"), None, None, None, None),
        P(("band", "req"), None, None),
        P(),
        P(),
    )
    out_specs = P("req", "band", None, None)
    return jax.shard_map(shards, mesh=mesh, in_specs=in_specs, out_specs=out_specs, check_vma=False)
```

```python
import jax
import jax.numpy as jnp
from jax import lax
from jax.experimental import pallas as pl
from jax.sharding import PartitionSpec as P

G = 32


def with_halo(x, sides, width):
    for axis, dim in sides:
        count, length = (lax.axis_size(axis), x.shape[dim])
        up = [(i, (i + 1) % count) for i in range(count - 1)]
        down = [(j, i) for i, j in up]
        last = lax.slice_in_dim(x, length - width, length, axis=dim)
        initial = lax.slice_in_dim(x, 0, width, axis=dim)
        before = lax.ppermute(last, axis, up)
        after = lax.ppermute(initial, axis, down)
        x = jnp.concatenate([before, x, after], axis=dim)
    return x


def exchange(value, axis):
    count = lax.axis_size(axis)
    spread = jnp.broadcast_to(value[None], (count,) + value.shape)
    return lax.all_to_all(spread, axis, 0, 0, tiled=True)


def norm_stats(field, groups):
    field = field.astype(jnp.float32)
    requests, rows, width, channels = field.shape
    grouped = field.reshape(requests, rows, width, groups, channels // groups)
    count = rows * width * (channels // groups)
    local_mean = jnp.sum(grouped, axis=(1, 2, 4)) / count
    deviation = grouped - local_mean[:, None, None, :, None]
    local_m2 = jnp.sum(deviation * deviation, axis=(1, 2, 4))
    stats = exchange(jnp.stack([local_mean, local_m2]), "band")
    means, m2s = stats[:, 0], stats[:, 1]
    bands = means.shape[0]
    mean = jnp.sum(means, axis=0) / bands
    gap = means - mean[None]
    m2 = jnp.sum(m2s, axis=0) + count * jnp.sum(gap * gap, axis=0)
    spread = m2 / (count * bands)
    return mean, lax.rsqrt(spread + 1e-05)


def norm_silu(field, mean, scale, groups):
    field = field.astype(jnp.float32)
    requests, rows, width, channels = field.shape
    grouped = field.reshape(requests, rows, width, groups, channels // groups)
    normed = (grouped - mean[:, None, None, :, None]) * scale[:, None, None, :, None]
    return jax.nn.silu(normed.reshape(field.shape)).astype(jnp.bfloat16)


def conv_input(field, groups):
    extended = with_halo(field, (("band", 1),), 1)
    mean, scale = norm_stats(field, groups)
    normed = norm_silu(extended, mean, scale, groups)
    band, bands = lax.axis_index("band"), lax.axis_size("band")
    row = lax.broadcasted_iota(jnp.int32, (1, normed.shape[1], 1, 1), 1)
    outside = ((row == 0) & (band == 0)) | ((row == normed.shape[1] - 1) & (band == bands - 1))
    normed = jnp.where(outside, jnp.zeros((), normed.dtype), normed)
    return jnp.pad(normed, ((0, 0), (0, 0), (1, 1), (0, 0)))


def taps_by_column(padded):
    width = padded.shape[1] - 2
    return jnp.concatenate([padded[:, tap : tap + width] for tap in range(3)], axis=-1)


def first_conv_kernel(x_ref, w_ref, u_ref, s_ref, o_ref):
    row = pl.program_id(0)
    total = None
    for tap in range(3):
        t = jnp.dot(x_ref[row + tap], w_ref[tap], preferred_element_type=jnp.float32)
        total = t if total is None else total + t
    rank = u_ref.shape[0]
    low = total[:, :rank]
    main = total[:, w_ref.shape[-1] - o_ref.shape[-1] :]
    lifted = jnp.dot(low.astype(jnp.bfloat16), u_ref[...], preferred_element_type=jnp.float32)
    o_ref[0] = main + lifted + s_ref[...]


def second_conv_kernel(x_ref, w_ref, r_ref, o_ref):
    row = pl.program_id(0)
    total = None
    for tap in range(3):
        t = jnp.dot(x_ref[row + tap], w_ref[tap], preferred_element_type=jnp.float32)
        total = t if total is None else total + t
    o_ref[0] = (r_ref[0].astype(jnp.float32) + total).astype(o_ref.dtype)


def first_conv(cols, weight, down, up, shift):
    rows, width, wide = cols.shape[0] - 2, cols.shape[1], cols.shape[2]
    out = weight.shape[-1]
    rank = down.shape[-1]
    lead = -(-rank // 128) * 128
    gap = jnp.zeros(down.shape[:-1] + (lead - rank,), down.dtype)
    weight = jnp.concatenate([down, gap, weight], axis=-1)
    flops = 2 * rows * width * wide * (out + lead) + 2 * rows * width * rank * out
    return pl.pallas_call(
        first_conv_kernel,
        grid=(rows,),
        in_specs=[
            pl.BlockSpec(cols.shape, lambda h: (0, 0, 0)),
            pl.BlockSpec(weight.shape, lambda h: (0, 0, 0)),
            pl.BlockSpec(up.shape, lambda h: (0, 0)),
            pl.BlockSpec(shift.shape, lambda h: (0, 0)),
        ],
        out_specs=pl.BlockSpec((1, width, out), lambda h: (h, 0, 0)),
        out_shape=jax.ShapeDtypeStruct((rows, width, out), jnp.float32),
        cost_estimate=pl.CostEstimate(
            flops=flops, transcendentals=0,
            bytes_accessed=cols.size * 2 + weight.size * 2 + rows * width * out * 4,
        ),
    )(cols, weight, up, shift)


def second_conv(cols, weight, residual):
    rows, width, wide = cols.shape[0] - 2, cols.shape[1], cols.shape[2]
    out = weight.shape[-1]
    return pl.pallas_call(
        second_conv_kernel,
        grid=(rows,),
        in_specs=[
            pl.BlockSpec(cols.shape, lambda h: (0, 0, 0)),
            pl.BlockSpec(weight.shape, lambda h: (0, 0, 0)),
            pl.BlockSpec((1, width, out), lambda h: (h, 0, 0)),
        ],
        out_specs=pl.BlockSpec((1, width, out), lambda h: (h, 0, 0)),
        out_shape=jax.ShapeDtypeStruct((rows, width, out), residual.dtype),
        cost_estimate=pl.CostEstimate(
            flops=2 * rows * width * wide * out, transcendentals=0,
            bytes_accessed=cols.size * 2 + weight.size * 2 + rows * width * out * 4,
        ),
    )(cols, weight, residual)


def fetch_adapter(slots, down, up):
    bands, reqs = lax.axis_size("band"), lax.axis_size("req")
    flat = jnp.concatenate([down.reshape(-1), up.reshape(-1)])
    lanes, sublanes = 128, 16
    piece_rows = -(-flat.size // (bands * lanes * sublanes)) * sublanes
    flat = jnp.pad(flat, (0, bands * piece_rows * lanes - flat.size))
    pieces = flat.reshape(bands, piece_rows, lanes)
    by_band = lax.all_to_all(pieces, "band", 0, 0, tiled=True)
    wanted = jnp.take(by_band, slots // reqs, axis=0)
    by_req = lax.all_to_all(wanted, "req", 0, 0, tiled=True)
    own = lax.axis_index("req")
    mine = lax.dynamic_index_in_dim(by_req, slots[own] % reqs, 0, keepdims=False)
    whole = exchange(mine, "band").reshape(-1)
    down_size = down.size
    chosen_down = whole[:down_size].reshape(down.shape[1:])
    chosen_up = whole[down_size : down_size + up.size].reshape(up.shape[1:])
    return chosen_down, chosen_up


def shards(
    latents,
    request_time_embedding,
    request_adapter,
    adapter_stored_row,
    first_conv_weight,
    stored_down_weight,
    stored_up_weight,
    second_conv_weight,
    time_projection_weight,
):
    requests, rows, width, channels = latents.shape
    every_adapter = exchange(request_adapter[0, 0], "req")
    slots = jnp.take(adapter_stored_row, every_adapter, axis=0)
    chosen_down, chosen_up = fetch_adapter(slots, stored_down_weight, stored_up_weight)
    shift = jnp.dot(
        jax.nn.silu(request_time_embedding.astype(jnp.float32)).astype(jnp.bfloat16),
        time_projection_weight,
        preferred_element_type=jnp.float32,
    )
    wide = 3 * channels
    hidden = first_conv(
        taps_by_column(conv_input(latents, G)[0]),
        first_conv_weight.reshape(3, wide, channels),
        chosen_down.reshape(3, wide, chosen_down.shape[-1]),
        chosen_up,
        shift,
    )[None]
    result = second_conv(
        taps_by_column(conv_input(hidden, G)[0]),
        second_conv_weight.reshape(3, wide, channels),
        latents[0],
    )
    return result[None]


def solution(mesh):
    in_specs = (
        P("req", "band", None, None),
        P("req", None),
        P("req", None),
        P(),
        P(),
        P(("band", "req"), None, None, None, None),
        P(("band", "req"), None, None),
        P(),
        P(),
    )
    out_specs = P("req", "band", None, None)
    return jax.shard_map(shards, mesh=mesh, in_specs=in_specs, out_specs=out_specs, check_vma=False)
```

```python
import jax
import jax.numpy as jnp
from jax import lax
from jax.experimental import pallas as pl
from jax.sharding import PartitionSpec as P

G = 32


def with_halo(x, sides, width):
    for axis, dim in sides:
        count, length = (lax.axis_size(axis), x.shape[dim])
        up = [(i, (i + 1) % count) for i in range(count - 1)]
        down = [(j, i) for i, j in up]
        last = lax.slice_in_dim(x, length - width, length, axis=dim)
        initial = lax.slice_in_dim(x, 0, width, axis=dim)
        before = lax.ppermute(last, axis, up)
        after = lax.ppermute(initial, axis, down)
        x = jnp.concatenate([before, x, after], axis=dim)
    return x


def exchange(value, axis):
    count = lax.axis_size(axis)
    spread = jnp.broadcast_to(value[None], (count,) + value.shape)
    return lax.all_to_all(spread, axis, 0, 0, tiled=True)


def norm_stats(field, groups):
    field = field.astype(jnp.float32)
    requests, rows, width, channels = field.shape
    grouped = field.reshape(requests, rows, width, groups, channels // groups)
    count = rows * width * (channels // groups)
    local_mean = jnp.sum(grouped, axis=(1, 2, 4)) / count
    deviation = grouped - local_mean[:, None, None, :, None]
    local_m2 = jnp.sum(deviation * deviation, axis=(1, 2, 4))
    stats = exchange(jnp.stack([local_mean, local_m2]), "band")
    means, m2s = stats[:, 0], stats[:, 1]
    bands = means.shape[0]
    mean = jnp.sum(means, axis=0) / bands
    gap = means - mean[None]
    m2 = jnp.sum(m2s, axis=0) + count * jnp.sum(gap * gap, axis=0)
    spread = m2 / (count * bands)
    return mean, lax.rsqrt(spread + 1e-05)


def norm_silu(field, mean, scale, groups):
    field = field.astype(jnp.float32)
    requests, rows, width, channels = field.shape
    grouped = field.reshape(requests, rows, width, groups, channels // groups)
    normed = (grouped - mean[:, None, None, :, None]) * scale[:, None, None, :, None]
    return jax.nn.silu(normed.reshape(field.shape)).astype(jnp.bfloat16)


def conv_input(field, groups):
    mean, scale = norm_stats(field, groups)
    extended = with_halo(norm_silu(field, mean, scale, groups), (("band", 1),), 1)
    return jnp.pad(extended, ((0, 0), (0, 0), (1, 1), (0, 0)))


def taps_by_column(padded):
    width = padded.shape[1] - 2
    return jnp.concatenate([padded[:, tap : tap + width] for tap in range(3)], axis=-1)


def first_conv_kernel(x_ref, w_ref, u_ref, s_ref, o_ref):
    row = pl.program_id(0)
    total = None
    for tap in range(3):
        t = jnp.dot(x_ref[row + tap], w_ref[tap], preferred_element_type=jnp.float32)
        total = t if total is None else total + t
    rank = u_ref.shape[0]
    low = total[:, :rank]
    main = total[:, w_ref.shape[-1] - o_ref.shape[-1] :]
    lifted = jnp.dot(low.astype(jnp.bfloat16), u_ref[...], preferred_element_type=jnp.float32)
    o_ref[0] = main + lifted + s_ref[...]


def second_conv_kernel(x_ref, w_ref, r_ref, o_ref):
    row = pl.program_id(0)
    total = None
    for tap in range(3):
        t = jnp.dot(x_ref[row + tap], w_ref[tap], preferred_element_type=jnp.float32)
        total = t if total is None else total + t
    o_ref[0] = (r_ref[0].astype(jnp.float32) + total).astype(o_ref.dtype)


def first_conv(cols, weight, down, up, shift):
    rows, width, wide = cols.shape[0] - 2, cols.shape[1], cols.shape[2]
    out = weight.shape[-1]
    rank = down.shape[-1]
    lead = -(-rank // 128) * 128
    gap = jnp.zeros(down.shape[:-1] + (lead - rank,), down.dtype)
    weight = jnp.concatenate([down, gap, weight], axis=-1)
    flops = 2 * rows * width * wide * (out + lead) + 2 * rows * width * rank * out
    return pl.pallas_call(
        first_conv_kernel,
        grid=(rows,),
        in_specs=[
            pl.BlockSpec(cols.shape, lambda h: (0, 0, 0)),
            pl.BlockSpec(weight.shape, lambda h: (0, 0, 0)),
            pl.BlockSpec(up.shape, lambda h: (0, 0)),
            pl.BlockSpec(shift.shape, lambda h: (0, 0)),
        ],
        out_specs=pl.BlockSpec((1, width, out), lambda h: (h, 0, 0)),
        out_shape=jax.ShapeDtypeStruct((rows, width, out), jnp.float32),
        cost_estimate=pl.CostEstimate(
            flops=flops, transcendentals=0,
            bytes_accessed=cols.size * 2 + weight.size * 2 + rows * width * out * 4,
        ),
    )(cols, weight, up, shift)


def second_conv(cols, weight, residual):
    rows, width, wide = cols.shape[0] - 2, cols.shape[1], cols.shape[2]
    out = weight.shape[-1]
    return pl.pallas_call(
        second_conv_kernel,
        grid=(rows,),
        in_specs=[
            pl.BlockSpec(cols.shape, lambda h: (0, 0, 0)),
            pl.BlockSpec(weight.shape, lambda h: (0, 0, 0)),
            pl.BlockSpec((1, width, out), lambda h: (h, 0, 0)),
        ],
        out_specs=pl.BlockSpec((1, width, out), lambda h: (h, 0, 0)),
        out_shape=jax.ShapeDtypeStruct((rows, width, out), residual.dtype),
        cost_estimate=pl.CostEstimate(
            flops=2 * rows * width * wide * out, transcendentals=0,
            bytes_accessed=cols.size * 2 + weight.size * 2 + rows * width * out * 4,
        ),
    )(cols, weight, residual)


def fetch_adapter(slots, down, up):
    bands, reqs = lax.axis_size("band"), lax.axis_size("req")
    flat = jnp.concatenate([down.reshape(-1), up.reshape(-1)])
    lanes, sublanes = 128, 16
    piece_rows = -(-flat.size // (bands * lanes * sublanes)) * sublanes
    flat = jnp.pad(flat, (0, bands * piece_rows * lanes - flat.size))
    pieces = flat.reshape(bands, piece_rows, lanes)
    by_band = lax.all_to_all(pieces, "band", 0, 0, tiled=True)
    wanted = jnp.take(by_band, slots // reqs, axis=0)
    by_req = lax.all_to_all(wanted, "req", 0, 0, tiled=True)
    own = lax.axis_index("req")
    mine = lax.dynamic_index_in_dim(by_req, slots[own] % reqs, 0, keepdims=False)
    whole = exchange(mine, "band").reshape(-1)
    down_size = down.size
    chosen_down = whole[:down_size].reshape(down.shape[1:])
    chosen_up = whole[down_size : down_size + up.size].reshape(up.shape[1:])
    return chosen_down, chosen_up


def shards(
    latents,
    request_time_embedding,
    request_adapter,
    adapter_stored_row,
    first_conv_weight,
    stored_down_weight,
    stored_up_weight,
    second_conv_weight,
    time_projection_weight,
):
    requests, rows, width, channels = latents.shape
    every_adapter = exchange(request_adapter[0, 0], "req")
    slots = jnp.take(adapter_stored_row, every_adapter, axis=0)
    chosen_down, chosen_up = fetch_adapter(slots, stored_down_weight, stored_up_weight)
    shift = jnp.dot(
        jax.nn.silu(request_time_embedding.astype(jnp.float32)).astype(jnp.bfloat16),
        time_projection_weight,
        preferred_element_type=jnp.float32,
    )
    wide = 3 * channels
    hidden = first_conv(
        taps_by_column(conv_input(latents, G)[0]),
        first_conv_weight.reshape(3, wide, channels),
        chosen_down.reshape(3, wide, chosen_down.shape[-1]),
        chosen_up,
        shift,
    )[None]
    result = second_conv(
        taps_by_column(conv_input(hidden, G)[0]),
        second_conv_weight.reshape(3, wide, channels),
        latents[0],
    )
    return result[None]


def solution(mesh):
    in_specs = (
        P("req", "band", None, None),
        P("req", None),
        P("req", None),
        P(),
        P(),
        P(("band", "req"), None, None, None, None),
        P(("band", "req"), None, None),
        P(),
        P(),
    )
    out_specs = P("req", "band", None, None)
    return jax.shard_map(shards, mesh=mesh, in_specs=in_specs, out_specs=out_specs, check_vma=False)
```

```python
import jax
import jax.numpy as jnp
from jax import lax
from jax.experimental import pallas as pl
from jax.sharding import PartitionSpec as P

G = 32


def with_halo(x, sides, width):
    for axis, dim in sides:
        count, length = (lax.axis_size(axis), x.shape[dim])
        up = [(i, (i + 1) % count) for i in range(count - 1)]
        down = [(j, i) for i, j in up]
        last = lax.slice_in_dim(x, length - width, length, axis=dim)
        initial = lax.slice_in_dim(x, 0, width, axis=dim)
        before = lax.ppermute(last, axis, up)
        after = lax.ppermute(initial, axis, down)
        x = jnp.concatenate([before, x, after], axis=dim)
    return x


def exchange(value, axis):
    count = lax.axis_size(axis)
    spread = jnp.broadcast_to(value[None], (count,) + value.shape)
    return lax.all_to_all(spread, axis, 0, 0, tiled=True)


def norm_stats(field, groups):
    field = field.astype(jnp.float32)
    requests, rows, width, channels = field.shape
    grouped = field.reshape(requests, rows, width, groups, channels // groups)
    count = rows * width * (channels // groups)
    local_mean = jnp.sum(grouped, axis=(1, 2, 4)) / count
    deviation = grouped - local_mean[:, None, None, :, None]
    local_m2 = jnp.sum(deviation * deviation, axis=(1, 2, 4))
    stats = exchange(jnp.stack([local_mean, local_m2]), "band")
    means, m2s = stats[:, 0], stats[:, 1]
    bands = means.shape[0]
    mean = jnp.sum(means, axis=0) / bands
    gap = means - mean[None]
    m2 = jnp.sum(m2s, axis=0) + count * jnp.sum(gap * gap, axis=0)
    spread = m2 / (count * bands)
    return mean, lax.rsqrt(spread + 1e-05)


def norm_silu(field, mean, scale, groups):
    field = field.astype(jnp.float32)
    requests, rows, width, channels = field.shape
    grouped = field.reshape(requests, rows, width, groups, channels // groups)
    normed = (grouped - mean[:, None, None, :, None]) * scale[:, None, None, :, None]
    return jax.nn.silu(normed.reshape(field.shape)).astype(jnp.bfloat16)


def conv_input(field, groups):
    mean, scale = norm_stats(field, groups)
    return with_halo(norm_silu(field, mean, scale, groups), (("band", 1),), 1)


def taps_by_column(field):
    none = (0, 0)
    left = jnp.pad(field[:, :-1], (none, (1, 0), none))
    right = jnp.pad(field[:, 1:], (none, (0, 1), none))
    return jnp.concatenate([left, field, right], axis=-1)


def first_conv_kernel(x_ref, w_ref, u_ref, s_ref, o_ref):
    row = pl.program_id(0)
    total = None
    for tap in range(3):
        t = jnp.dot(x_ref[row + tap], w_ref[tap], preferred_element_type=jnp.float32)
        total = t if total is None else total + t
    rank = u_ref.shape[0]
    low = total[:, :rank]
    main = total[:, w_ref.shape[-1] - o_ref.shape[-1] :]
    lifted = jnp.dot(low.astype(jnp.bfloat16), u_ref[...], preferred_element_type=jnp.float32)
    o_ref[0] = main + lifted + s_ref[...]


def second_conv_kernel(x_ref, w_ref, r_ref, o_ref):
    row = pl.program_id(0)
    total = None
    for tap in range(3):
        t = jnp.dot(x_ref[row + tap], w_ref[tap], preferred_element_type=jnp.float32)
        total = t if total is None else total + t
    o_ref[0] = (r_ref[0].astype(jnp.float32) + total).astype(o_ref.dtype)


def first_conv(cols, weight, down, up, shift):
    rows, width, wide = cols.shape[0] - 2, cols.shape[1], cols.shape[2]
    out = weight.shape[-1]
    rank = down.shape[-1]
    lead = -(-rank // 128) * 128
    gap = jnp.zeros(down.shape[:-1] + (lead - rank,), down.dtype)
    weight = jnp.concatenate([down, gap, weight], axis=-1)
    flops = 2 * rows * width * wide * (out + lead) + 2 * rows * width * rank * out
    return pl.pallas_call(
        first_conv_kernel,
        grid=(rows,),
        in_specs=[
            pl.BlockSpec(cols.shape, lambda h: (0, 0, 0)),
            pl.BlockSpec(weight.shape, lambda h: (0, 0, 0)),
            pl.BlockSpec(up.shape, lambda h: (0, 0)),
            pl.BlockSpec(shift.shape, lambda h: (0, 0)),
        ],
        out_specs=pl.BlockSpec((1, width, out), lambda h: (h, 0, 0)),
        out_shape=jax.ShapeDtypeStruct((rows, width, out), jnp.float32),
        cost_estimate=pl.CostEstimate(
            flops=flops, transcendentals=0,
            bytes_accessed=cols.size * 2 + weight.size * 2 + rows * width * out * 4,
        ),
    )(cols, weight, up, shift)


def second_conv(cols, weight, residual):
    rows, width, wide = cols.shape[0] - 2, cols.shape[1], cols.shape[2]
    out = weight.shape[-1]
    return pl.pallas_call(
        second_conv_kernel,
        grid=(rows,),
        in_specs=[
            pl.BlockSpec(cols.shape, lambda h: (0, 0, 0)),
            pl.BlockSpec(weight.shape, lambda h: (0, 0, 0)),
            pl.BlockSpec((1, width, out), lambda h: (h, 0, 0)),
        ],
        out_specs=pl.BlockSpec((1, width, out), lambda h: (h, 0, 0)),
        out_shape=jax.ShapeDtypeStruct((rows, width, out), residual.dtype),
        cost_estimate=pl.CostEstimate(
            flops=2 * rows * width * wide * out, transcendentals=0,
            bytes_accessed=cols.size * 2 + weight.size * 2 + rows * width * out * 4,
        ),
    )(cols, weight, residual)


def fetch_adapter(slots, down, up):
    bands, reqs = lax.axis_size("band"), lax.axis_size("req")
    flat = jnp.concatenate([down.reshape(-1), up.reshape(-1)])
    lanes, sublanes = 128, 16
    piece_rows = -(-flat.size // (bands * lanes * sublanes)) * sublanes
    flat = jnp.pad(flat, (0, bands * piece_rows * lanes - flat.size))
    pieces = flat.reshape(bands, piece_rows, lanes)
    by_band = lax.all_to_all(pieces, "band", 0, 0, tiled=True)
    wanted = jnp.take(by_band, slots // reqs, axis=0)
    by_req = lax.all_to_all(wanted, "req", 0, 0, tiled=True)
    own = lax.axis_index("req")
    mine = lax.dynamic_index_in_dim(by_req, slots[own] % reqs, 0, keepdims=False)
    whole = exchange(mine, "band").reshape(-1)
    down_size = down.size
    chosen_down = whole[:down_size].reshape(down.shape[1:])
    chosen_up = whole[down_size : down_size + up.size].reshape(up.shape[1:])
    return chosen_down, chosen_up


def shards(
    latents,
    request_time_embedding,
    request_adapter,
    adapter_stored_row,
    first_conv_weight,
    stored_down_weight,
    stored_up_weight,
    second_conv_weight,
    time_projection_weight,
):
    requests, rows, width, channels = latents.shape
    every_adapter = exchange(request_adapter[0, 0], "req")
    slots = jnp.take(adapter_stored_row, every_adapter, axis=0)
    chosen_down, chosen_up = fetch_adapter(slots, stored_down_weight, stored_up_weight)
    shift = jnp.dot(
        jax.nn.silu(request_time_embedding.astype(jnp.float32)).astype(jnp.bfloat16),
        time_projection_weight,
        preferred_element_type=jnp.float32,
    )
    wide = 3 * channels
    hidden = first_conv(
        taps_by_column(conv_input(latents, G)[0]),
        first_conv_weight.reshape(3, wide, channels),
        chosen_down.reshape(3, wide, chosen_down.shape[-1]),
        chosen_up,
        shift,
    )[None]
    result = second_conv(
        taps_by_column(conv_input(hidden, G)[0]),
        second_conv_weight.reshape(3, wide, channels),
        latents[0],
    )
    return result[None]


def solution(mesh):
    in_specs = (
        P("req", "band", None, None),
        P("req", None),
        P("req", None),
        P(),
        P(),
        P(("band", "req"), None, None, None, None),
        P(("band", "req"), None, None),
        P(),
        P(),
    )
    out_specs = P("req", "band", None, None)
    return jax.shard_map(shards, mesh=mesh, in_specs=in_specs, out_specs=out_specs, check_vma=False)
```

```python
import jax
import jax.numpy as jnp
from jax import lax
from jax.experimental import pallas as pl
from jax.sharding import PartitionSpec as P

G = 32


def with_halo(x, sides, width):
    for axis, dim in sides:
        count, length = (lax.axis_size(axis), x.shape[dim])
        up = [(i, (i + 1) % count) for i in range(count - 1)]
        down = [(j, i) for i, j in up]
        last = lax.slice_in_dim(x, length - width, length, axis=dim)
        initial = lax.slice_in_dim(x, 0, width, axis=dim)
        before = lax.ppermute(last, axis, up)
        after = lax.ppermute(initial, axis, down)
        x = jnp.concatenate([before, x, after], axis=dim)
    return x


def exchange(value, axis):
    count = lax.axis_size(axis)
    spread = jnp.broadcast_to(value[None], (count,) + value.shape)
    return lax.all_to_all(spread, axis, 0, 0, tiled=True)


def norm_stats(field, groups):
    field = field.astype(jnp.float32)
    requests, rows, channels, width = field.shape
    grouped = field.reshape(requests, rows, groups, channels // groups, width)
    count = rows * width * (channels // groups)
    local_mean = jnp.sum(grouped, axis=(1, 3, 4)) / count
    deviation = grouped - local_mean[:, None, :, None, None]
    local_m2 = jnp.sum(deviation * deviation, axis=(1, 3, 4))
    stats = exchange(jnp.stack([local_mean, local_m2]), "band")
    means, m2s = stats[:, 0], stats[:, 1]
    bands = means.shape[0]
    mean = jnp.sum(means, axis=0) / bands
    gap = means - mean[None]
    m2 = jnp.sum(m2s, axis=0) + count * jnp.sum(gap * gap, axis=0)
    spread = m2 / (count * bands)
    return mean, lax.rsqrt(spread + 1e-05)


def norm_silu(field, mean, scale, groups):
    field = field.astype(jnp.float32)
    requests, rows, channels, width = field.shape
    grouped = field.reshape(requests, rows, groups, channels // groups, width)
    normed = (grouped - mean[:, None, :, None, None]) * scale[:, None, :, None, None]
    return jax.nn.silu(normed.reshape(field.shape)).astype(jnp.bfloat16)


def conv_input(field, groups):
    mean, scale = norm_stats(field, groups)
    return with_halo(norm_silu(field, mean, scale, groups), (("band", 1),), 1)


def taps_by_column(field):
    none = (0, 0)
    left = jnp.pad(field[:, :, :-1], (none, none, (1, 0)))
    right = jnp.pad(field[:, :, 1:], (none, none, (0, 1)))
    return jnp.concatenate([left, field, right], axis=1)


def tap_weights(kernel):
    taps, cols, inner, outer = kernel.shape
    return jnp.transpose(kernel, (0, 3, 1, 2)).reshape(taps, outer, cols * inner)


def first_conv_kernel(x_ref, w_ref, u_ref, s_ref, o_ref):
    row = pl.program_id(0)
    total = None
    for tap in range(3):
        t = jnp.dot(w_ref[tap], x_ref[row + tap], preferred_element_type=jnp.float32)
        total = t if total is None else total + t
    rank = u_ref.shape[1]
    low = total[:rank]
    main = total[w_ref.shape[1] - o_ref.shape[1] :]
    lifted = jnp.dot(u_ref[...], low.astype(jnp.bfloat16), preferred_element_type=jnp.float32)
    o_ref[0] = main + lifted + s_ref[...]


def second_conv_kernel(x_ref, w_ref, r_ref, o_ref):
    row = pl.program_id(0)
    total = None
    for tap in range(3):
        t = jnp.dot(w_ref[tap], x_ref[row + tap], preferred_element_type=jnp.float32)
        total = t if total is None else total + t
    o_ref[0] = (r_ref[0].astype(jnp.float32) + total).astype(o_ref.dtype)


def first_conv(cols, weight, down, up_t, shift):
    rows, wide, width = cols.shape[0] - 2, cols.shape[1], cols.shape[2]
    out = weight.shape[1]
    rank = down.shape[1]
    lead = -(-rank // 128) * 128
    base = jnp.concatenate([jnp.zeros((3, lead, wide), weight.dtype), weight], axis=1)
    weight = lax.dynamic_update_slice(base, down, (0, 0, 0))
    flops = 2 * rows * width * wide * (out + lead) + 2 * rows * width * rank * out
    return pl.pallas_call(
        first_conv_kernel,
        grid=(rows,),
        in_specs=[
            pl.BlockSpec(cols.shape, lambda h: (0, 0, 0)),
            pl.BlockSpec(weight.shape, lambda h: (0, 0, 0)),
            pl.BlockSpec(up_t.shape, lambda h: (0, 0)),
            pl.BlockSpec(shift.shape, lambda h: (0, 0)),
        ],
        out_specs=pl.BlockSpec((1, out, width), lambda h: (h, 0, 0)),
        out_shape=jax.ShapeDtypeStruct((rows, out, width), jnp.float32),
        cost_estimate=pl.CostEstimate(
            flops=flops, transcendentals=0,
            bytes_accessed=cols.size * 2 + weight.size * 2 + rows * width * out * 4,
        ),
    )(cols, weight, up_t, shift)


def second_conv(cols, weight, residual):
    rows, wide, width = cols.shape[0] - 2, cols.shape[1], cols.shape[2]
    out = weight.shape[1]
    return pl.pallas_call(
        second_conv_kernel,
        grid=(rows,),
        in_specs=[
            pl.BlockSpec(cols.shape, lambda h: (0, 0, 0)),
            pl.BlockSpec(weight.shape, lambda h: (0, 0, 0)),
            pl.BlockSpec((1, out, width), lambda h: (h, 0, 0)),
        ],
        out_specs=pl.BlockSpec((1, out, width), lambda h: (h, 0, 0)),
        out_shape=jax.ShapeDtypeStruct((rows, out, width), residual.dtype),
        cost_estimate=pl.CostEstimate(
            flops=2 * rows * width * wide * out, transcendentals=0,
            bytes_accessed=cols.size * 2 + weight.size * 2 + rows * width * out * 4,
        ),
    )(cols, weight, residual)


def fetch_adapter(slots, down, up):
    bands, reqs = lax.axis_size("band"), lax.axis_size("req")
    flat = jnp.concatenate([down.reshape(-1), up.reshape(-1)])
    lanes, sublanes = 128, 16
    piece_rows = -(-flat.size // (bands * lanes * sublanes)) * sublanes
    flat = jnp.pad(flat, (0, bands * piece_rows * lanes - flat.size))
    pieces = flat.reshape(bands, piece_rows, lanes)
    by_band = lax.all_to_all(pieces, "band", 0, 0, tiled=True)
    wanted = jnp.take(by_band, slots // reqs, axis=0)
    by_req = lax.all_to_all(wanted, "req", 0, 0, tiled=True)
    own = lax.axis_index("req")
    mine = lax.dynamic_index_in_dim(by_req, slots[own] % reqs, 0, keepdims=False)
    whole = exchange(mine, "band").reshape(-1)
    down_size = down.size
    chosen_down = whole[:down_size].reshape(down.shape[1:])
    chosen_up = whole[down_size : down_size + up.size].reshape(up.shape[1:])
    return chosen_down, chosen_up


def shards(
    latents,
    request_time_embedding,
    request_adapter,
    adapter_stored_row,
    first_conv_weight,
    stored_down_weight,
    stored_up_weight,
    second_conv_weight,
    time_projection_weight,
):
    requests, rows, width, channels = latents.shape
    every_adapter = exchange(request_adapter[0, 0], "req")
    slots = jnp.take(adapter_stored_row, every_adapter, axis=0)
    chosen_down, chosen_up = fetch_adapter(slots, stored_down_weight, stored_up_weight)
    shift = jnp.dot(
        jax.nn.silu(request_time_embedding.astype(jnp.float32)).astype(jnp.bfloat16),
        time_projection_weight,
        preferred_element_type=jnp.float32,
    )
    field = jnp.swapaxes(latents, 2, 3)
    hidden = first_conv(
        taps_by_column(conv_input(field, G)[0]),
        tap_weights(first_conv_weight),
        tap_weights(chosen_down),
        chosen_up.T,
        shift.reshape(channels, 1),
    )[None]
    result = second_conv(
        taps_by_column(conv_input(hidden, G)[0]),
        tap_weights(second_conv_weight),
        field[0],
    )
    return jnp.swapaxes(result[None], 2, 3)


def solution(mesh):
    in_specs = (
        P("req", "band", None, None),
        P("req", None),
        P("req", None),
        P(),
        P(),
        P(("band", "req"), None, None, None, None),
        P(("band", "req"), None, None),
        P(),
        P(),
    )
    out_specs = P("req", "band", None, None)
    return jax.shard_map(shards, mesh=mesh, in_specs=in_specs, out_specs=out_specs, check_vma=False)
```

```python
import jax
import jax.numpy as jnp
from jax import lax
from jax.experimental import pallas as pl
from jax.sharding import PartitionSpec as P

G = 32


def with_halo(x, sides, width):
    for axis, dim in sides:
        count, length = (lax.axis_size(axis), x.shape[dim])
        up = [(i, (i + 1) % count) for i in range(count - 1)]
        down = [(j, i) for i, j in up]
        last = lax.slice_in_dim(x, length - width, length, axis=dim)
        initial = lax.slice_in_dim(x, 0, width, axis=dim)
        before = lax.ppermute(last, axis, up)
        after = lax.ppermute(initial, axis, down)
        x = jnp.concatenate([before, x, after], axis=dim)
    return x


def exchange(value, axis):
    count = lax.axis_size(axis)
    spread = jnp.broadcast_to(value[None], (count,) + value.shape)
    return lax.all_to_all(spread, axis, 0, 0, tiled=True)


def norm_stats(field, groups):
    field = field.astype(jnp.float32)
    requests, rows, channels, width = field.shape
    grouped = field.reshape(requests, rows, groups, channels // groups, width)
    count = rows * width * (channels // groups)
    local_mean = jnp.sum(grouped, axis=(1, 3, 4)) / count
    deviation = grouped - local_mean[:, None, :, None, None]
    local_m2 = jnp.sum(deviation * deviation, axis=(1, 3, 4))
    stats = exchange(jnp.stack([local_mean, local_m2]), "band")
    means, m2s = stats[:, 0], stats[:, 1]
    bands = means.shape[0]
    mean = jnp.sum(means, axis=0) / bands
    gap = means - mean[None]
    m2 = jnp.sum(m2s, axis=0) + count * jnp.sum(gap * gap, axis=0)
    spread = m2 / (count * bands)
    return mean, lax.rsqrt(spread + 1e-05)


def norm_silu(field, mean, scale, groups):
    field = field.astype(jnp.float32)
    requests, rows, channels, width = field.shape
    grouped = field.reshape(requests, rows, groups, channels // groups, width)
    normed = (grouped - mean[:, None, :, None, None]) * scale[:, None, :, None, None]
    return jax.nn.silu(normed.reshape(field.shape)).astype(jnp.bfloat16)


def conv_input(field, groups):
    mean, scale = norm_stats(field, groups)
    return with_halo(norm_silu(field, mean, scale, groups), (("band", 1),), 1)


def taps_by_column(field):
    none = (0, 0)
    left = jnp.pad(field[:, :, :-1], (none, none, (1, 0)))
    right = jnp.pad(field[:, :, 1:], (none, none, (0, 1)))
    return jnp.concatenate([left, field, right], axis=1)


def tap_weights(kernel):
    taps, cols, inner, outer = kernel.shape
    return jnp.transpose(kernel, (0, 3, 1, 2)).reshape(taps, outer, cols * inner)


def first_conv_kernel(x_ref, w_ref, u_ref, s_ref, k_ref, o_ref):
    row = pl.program_id(0)
    total = None
    for tap in range(3):
        t = jnp.dot(w_ref[tap], x_ref[row + tap], preferred_element_type=jnp.float32)
        total = t if total is None else total + t
    rank = u_ref.shape[1]
    low = total[:rank]
    main = total[w_ref.shape[1] - o_ref.shape[1] :]
    lifted = jnp.dot(u_ref[...], low.astype(jnp.bfloat16), preferred_element_type=jnp.float32)
    o_ref[0] = main + lifted + s_ref[...]


def second_conv_kernel(x_ref, w_ref, r_ref, o_ref):
    row = pl.program_id(0)
    total = None
    for tap in range(3):
        t = jnp.dot(w_ref[tap], x_ref[row + tap], preferred_element_type=jnp.float32)
        total = t if total is None else total + t
    o_ref[0] = (r_ref[0].astype(jnp.float32) + total).astype(o_ref.dtype)


def merged_base(weight, rank):
    lead = -(-rank // 128) * 128
    return jnp.concatenate([jnp.zeros((3, lead, weight.shape[2]), weight.dtype), weight], axis=1)


def first_conv(cols, base, down, up_t, shift, out, keep):
    rows, wide, width = cols.shape[0] - 2, cols.shape[1], cols.shape[2]
    rank = down.shape[1]
    lead = base.shape[1] - out
    weight = lax.dynamic_update_slice(base, down, (0, 0, 0))
    flops = 2 * rows * width * wide * (out + lead) + 2 * rows * width * rank * out
    return pl.pallas_call(
        first_conv_kernel,
        grid=(rows,),
        in_specs=[
            pl.BlockSpec(cols.shape, lambda h: (0, 0, 0)),
            pl.BlockSpec(weight.shape, lambda h: (0, 0, 0)),
            pl.BlockSpec(up_t.shape, lambda h: (0, 0)),
            pl.BlockSpec(shift.shape, lambda h: (0, 0)),
            pl.BlockSpec(memory_space=pl.ANY),
        ],
        out_specs=pl.BlockSpec((1, out, width), lambda h: (h, 0, 0)),
        out_shape=jax.ShapeDtypeStruct((rows, out, width), jnp.float32),
        cost_estimate=pl.CostEstimate(
            flops=flops, transcendentals=0,
            bytes_accessed=cols.size * 2 + weight.size * 2 + rows * width * out * 4,
        ),
    )(cols, weight, up_t, shift, keep)


def second_conv(cols, weight, residual):
    rows, wide, width = cols.shape[0] - 2, cols.shape[1], cols.shape[2]
    out = weight.shape[1]
    return pl.pallas_call(
        second_conv_kernel,
        grid=(rows,),
        in_specs=[
            pl.BlockSpec(cols.shape, lambda h: (0, 0, 0)),
            pl.BlockSpec(weight.shape, lambda h: (0, 0, 0)),
            pl.BlockSpec((1, out, width), lambda h: (h, 0, 0)),
        ],
        out_specs=pl.BlockSpec((1, out, width), lambda h: (h, 0, 0)),
        out_shape=jax.ShapeDtypeStruct((rows, out, width), residual.dtype),
        cost_estimate=pl.CostEstimate(
            flops=2 * rows * width * wide * out, transcendentals=0,
            bytes_accessed=cols.size * 2 + weight.size * 2 + rows * width * out * 4,
        ),
    )(cols, weight, residual)


def fetch_adapter(slots, down, up):
    bands, reqs = lax.axis_size("band"), lax.axis_size("req")
    flat = jnp.concatenate([down.reshape(-1), up.reshape(-1)])
    lanes, sublanes = 128, 16
    piece_rows = -(-flat.size // (bands * lanes * sublanes)) * sublanes
    flat = jnp.pad(flat, (0, bands * piece_rows * lanes - flat.size))
    pieces = flat.reshape(bands, piece_rows, lanes)
    by_band = lax.all_to_all(pieces, "band", 0, 0, tiled=True)
    wanted = jnp.take(by_band, slots // reqs, axis=0)
    by_req = lax.all_to_all(wanted, "req", 0, 0, tiled=True)
    own = lax.axis_index("req")
    mine = lax.dynamic_index_in_dim(by_req, slots[own] % reqs, 0, keepdims=False)
    whole = exchange(mine, "band").reshape(-1)
    down_size = down.size
    chosen_down = whole[:down_size].reshape(down.shape[1:])
    chosen_up = whole[down_size : down_size + up.size].reshape(up.shape[1:])
    return chosen_down, chosen_up


def shards(
    latents,
    request_time_embedding,
    request_adapter,
    adapter_stored_row,
    first_conv_weight,
    stored_down_weight,
    stored_up_weight,
    second_conv_weight,
    time_projection_weight,
):
    requests, rows, width, channels = latents.shape
    every_adapter = exchange(request_adapter[0, 0], "req")
    slots = jnp.take(adapter_stored_row, every_adapter, axis=0)
    chosen_down, chosen_up = fetch_adapter(slots, stored_down_weight, stored_up_weight)
    shift = jnp.dot(
        jax.nn.silu(request_time_embedding.astype(jnp.float32)).astype(jnp.bfloat16),
        time_projection_weight,
        preferred_element_type=jnp.float32,
    )
    field = jnp.swapaxes(latents, 2, 3)
    base = merged_base(tap_weights(first_conv_weight), chosen_down.shape[-1])
    second_weight = tap_weights(second_conv_weight)
    hidden = first_conv(
        taps_by_column(conv_input(field, G)[0]),
        base,
        tap_weights(chosen_down),
        chosen_up.T,
        shift.reshape(channels, 1),
        channels,
        second_weight,
    )[None]
    result = second_conv(taps_by_column(conv_input(hidden, G)[0]), second_weight, field[0])
    return jnp.swapaxes(result[None], 2, 3)


def solution(mesh):
    in_specs = (
        P("req", "band", None, None),
        P("req", None),
        P("req", None),
        P(),
        P(),
        P(("band", "req"), None, None, None, None),
        P(("band", "req"), None, None),
        P(),
        P(),
    )
    out_specs = P("req", "band", None, None)
    return jax.shard_map(shards, mesh=mesh, in_specs=in_specs, out_specs=out_specs, check_vma=False)
```

```python
import jax
import jax.numpy as jnp
from jax import lax
from jax.experimental import pallas as pl
from jax.sharding import PartitionSpec as P

G = 32


def with_halo(x, sides, width):
    for axis, dim in sides:
        count, length = (lax.axis_size(axis), x.shape[dim])
        up = [(i, (i + 1) % count) for i in range(count - 1)]
        down = [(j, i) for i, j in up]
        last = lax.slice_in_dim(x, length - width, length, axis=dim)
        initial = lax.slice_in_dim(x, 0, width, axis=dim)
        before = lax.ppermute(last, axis, up)
        after = lax.ppermute(initial, axis, down)
        x = jnp.concatenate([before, x, after], axis=dim)
    return x


def exchange(value, axis):
    count = lax.axis_size(axis)
    spread = jnp.broadcast_to(value[None], (count,) + value.shape)
    return lax.all_to_all(spread, axis, 0, 0, tiled=True)


def norm_stats(field, groups):
    field = field.astype(jnp.float32)
    requests, rows, channels, width = field.shape
    grouped = field.reshape(requests, rows, groups, channels // groups, width)
    count = rows * width * (channels // groups)
    local_mean = jnp.sum(grouped, axis=(1, 3, 4)) / count
    deviation = grouped - local_mean[:, None, :, None, None]
    local_m2 = jnp.sum(deviation * deviation, axis=(1, 3, 4))
    stats = exchange(jnp.stack([local_mean, local_m2]), "band")
    means, m2s = stats[:, 0], stats[:, 1]
    bands = means.shape[0]
    mean = jnp.sum(means, axis=0) / bands
    gap = means - mean[None]
    m2 = jnp.sum(m2s, axis=0) + count * jnp.sum(gap * gap, axis=0)
    spread = m2 / (count * bands)
    return mean, lax.rsqrt(spread + 1e-05)


def norm_silu(field, mean, scale, groups):
    field = field.astype(jnp.float32)
    requests, rows, channels, width = field.shape
    grouped = field.reshape(requests, rows, groups, channels // groups, width)
    normed = (grouped - mean[:, None, :, None, None]) * scale[:, None, :, None, None]
    return jax.nn.silu(normed.reshape(field.shape)).astype(jnp.bfloat16)


def conv_input(field, groups):
    mean, scale = norm_stats(field, groups)
    return with_halo(norm_silu(field, mean, scale, groups), (("band", 1),), 1)


def taps_by_column(field):
    none = (0, 0)
    left = jnp.pad(field[:, :, :-1], (none, none, (1, 0)))
    right = jnp.pad(field[:, :, 1:], (none, none, (0, 1)))
    return jnp.concatenate([left, field, right], axis=1)


def wide_of(kernel):
    return kernel.shape[1] * kernel.shape[2]


def tap_weights(kernel):
    taps, cols, inner, outer = kernel.shape
    return jnp.transpose(kernel, (0, 3, 1, 2)).reshape(taps, outer, cols * inner)


def first_conv_kernel(x_ref, w_ref, u_ref, s_ref, o_ref):
    row = pl.program_id(0)
    total = None
    for tap in range(3):
        t = jnp.dot(w_ref[tap], x_ref[row + tap], preferred_element_type=jnp.float32)
        total = t if total is None else total + t
    rank = u_ref.shape[1]
    low = total[:rank]
    main = total[w_ref.shape[1] - o_ref.shape[1] :]
    lifted = jnp.dot(u_ref[...], low.astype(jnp.bfloat16), preferred_element_type=jnp.float32)
    o_ref[0] = main + lifted + s_ref[...]


def second_conv_kernel(x_ref, w_ref, r_ref, o_ref):
    row = pl.program_id(0)
    total = None
    for tap in range(3):
        t = lax.dot_general(
            w_ref[tap], x_ref[row + tap], (((0,), (0,)), ((), ())), preferred_element_type=jnp.float32
        )
        total = t if total is None else total + t
    o_ref[0] = (r_ref[0].astype(jnp.float32) + total).astype(o_ref.dtype)


def first_conv(cols, weight, down, up_t, shift):
    rows, wide, width = cols.shape[0] - 2, cols.shape[1], cols.shape[2]
    out = weight.shape[1]
    rank = down.shape[1]
    lead = -(-rank // 128) * 128
    base = jnp.concatenate([jnp.zeros((3, lead, wide), weight.dtype), weight], axis=1)
    weight = lax.dynamic_update_slice(base, down, (0, 0, 0))
    flops = 2 * rows * width * wide * (out + lead) + 2 * rows * width * rank * out
    return pl.pallas_call(
        first_conv_kernel,
        grid=(rows,),
        in_specs=[
            pl.BlockSpec(cols.shape, lambda h: (0, 0, 0)),
            pl.BlockSpec(weight.shape, lambda h: (0, 0, 0)),
            pl.BlockSpec(up_t.shape, lambda h: (0, 0)),
            pl.BlockSpec(shift.shape, lambda h: (0, 0)),
        ],
        out_specs=pl.BlockSpec((1, out, width), lambda h: (h, 0, 0)),
        out_shape=jax.ShapeDtypeStruct((rows, out, width), jnp.float32),
        cost_estimate=pl.CostEstimate(
            flops=flops, transcendentals=0,
            bytes_accessed=cols.size * 2 + weight.size * 2 + rows * width * out * 4,
        ),
    )(cols, weight, up_t, shift)


def second_conv(cols, weight, residual):
    rows, wide, width = cols.shape[0] - 2, cols.shape[1], cols.shape[2]
    out = weight.shape[2]
    return pl.pallas_call(
        second_conv_kernel,
        grid=(rows,),
        in_specs=[
            pl.BlockSpec(cols.shape, lambda h: (0, 0, 0)),
            pl.BlockSpec(weight.shape, lambda h: (0, 0, 0)),
            pl.BlockSpec((1, out, width), lambda h: (h, 0, 0)),
        ],
        out_specs=pl.BlockSpec((1, out, width), lambda h: (h, 0, 0)),
        out_shape=jax.ShapeDtypeStruct((rows, out, width), residual.dtype),
        cost_estimate=pl.CostEstimate(
            flops=2 * rows * width * wide * out, transcendentals=0,
            bytes_accessed=cols.size * 2 + weight.size * 2 + rows * width * out * 4,
        ),
    )(cols, weight, residual)


def fetch_adapter(slots, down, up):
    bands, reqs = lax.axis_size("band"), lax.axis_size("req")
    flat = jnp.concatenate([down.reshape(-1), up.reshape(-1)])
    lanes, sublanes = 128, 16
    piece_rows = -(-flat.size // (bands * lanes * sublanes)) * sublanes
    flat = jnp.pad(flat, (0, bands * piece_rows * lanes - flat.size))
    pieces = flat.reshape(bands, piece_rows, lanes)
    by_band = lax.all_to_all(pieces, "band", 0, 0, tiled=True)
    wanted = jnp.take(by_band, slots // reqs, axis=0)
    by_req = lax.all_to_all(wanted, "req", 0, 0, tiled=True)
    own = lax.axis_index("req")
    mine = lax.dynamic_index_in_dim(by_req, slots[own] % reqs, 0, keepdims=False)
    whole = exchange(mine, "band").reshape(-1)
    down_size = down.size
    chosen_down = whole[:down_size].reshape(down.shape[1:])
    chosen_up = whole[down_size : down_size + up.size].reshape(up.shape[1:])
    return chosen_down, chosen_up


def shards(
    latents,
    request_time_embedding,
    request_adapter,
    adapter_stored_row,
    first_conv_weight,
    stored_down_weight,
    stored_up_weight,
    second_conv_weight,
    time_projection_weight,
):
    requests, rows, width, channels = latents.shape
    every_adapter = exchange(request_adapter[0, 0], "req")
    slots = jnp.take(adapter_stored_row, every_adapter, axis=0)
    chosen_down, chosen_up = fetch_adapter(slots, stored_down_weight, stored_up_weight)
    shift = jnp.dot(
        jax.nn.silu(request_time_embedding.astype(jnp.float32)).astype(jnp.bfloat16),
        time_projection_weight,
        preferred_element_type=jnp.float32,
    )
    field = jnp.swapaxes(latents, 2, 3)
    hidden = first_conv(
        taps_by_column(conv_input(field, G)[0]),
        tap_weights(first_conv_weight),
        tap_weights(chosen_down),
        chosen_up.T,
        shift.reshape(channels, 1),
    )[None]
    result = second_conv(
        taps_by_column(conv_input(hidden, G)[0]),
        second_conv_weight.reshape(3, wide_of(second_conv_weight), channels),
        field[0],
    )
    return jnp.swapaxes(result[None], 2, 3)


def solution(mesh):
    in_specs = (
        P("req", "band", None, None),
        P("req", None),
        P("req", None),
        P(),
        P(),
        P(("band", "req"), None, None, None, None),
        P(("band", "req"), None, None),
        P(),
        P(),
    )
    out_specs = P("req", "band", None, None)
    return jax.shard_map(shards, mesh=mesh, in_specs=in_specs, out_specs=out_specs, check_vma=False)
```

```python
import jax
import jax.numpy as jnp
from jax import lax
from jax.experimental import pallas as pl
from jax.sharding import PartitionSpec as P

G = 32


def with_halo(x, sides, width):
    for axis, dim in sides:
        count, length = (lax.axis_size(axis), x.shape[dim])
        up = [(i, (i + 1) % count) for i in range(count - 1)]
        down = [(j, i) for i, j in up]
        last = lax.slice_in_dim(x, length - width, length, axis=dim)
        initial = lax.slice_in_dim(x, 0, width, axis=dim)
        before = lax.ppermute(last, axis, up)
        after = lax.ppermute(initial, axis, down)
        x = jnp.concatenate([before, x, after], axis=dim)
    return x


def exchange(value, axis):
    count = lax.axis_size(axis)
    spread = jnp.broadcast_to(value[None], (count,) + value.shape)
    return lax.all_to_all(spread, axis, 0, 0, tiled=True)


def norm_stats(field, groups):
    field = field.astype(jnp.float32)
    requests, rows, channels, width = field.shape
    grouped = field.reshape(requests, rows, groups, channels // groups, width)
    count = rows * width * (channels // groups)
    local_mean = jnp.sum(grouped, axis=(1, 3, 4)) / count
    deviation = grouped - local_mean[:, None, :, None, None]
    local_m2 = jnp.sum(deviation * deviation, axis=(1, 3, 4))
    stats = exchange(jnp.stack([local_mean, local_m2]), "band")
    means, m2s = stats[:, 0], stats[:, 1]
    bands = means.shape[0]
    mean = jnp.sum(means, axis=0) / bands
    gap = means - mean[None]
    m2 = jnp.sum(m2s, axis=0) + count * jnp.sum(gap * gap, axis=0)
    spread = m2 / (count * bands)
    return mean, lax.rsqrt(spread + 1e-05)


def norm_silu(field, mean, scale, groups):
    field = field.astype(jnp.float32)
    requests, rows, channels, width = field.shape
    grouped = field.reshape(requests, rows, groups, channels // groups, width)
    normed = (grouped - mean[:, None, :, None, None]) * scale[:, None, :, None, None]
    return jax.nn.silu(normed.reshape(field.shape)).astype(jnp.bfloat16)


def conv_input(field, groups):
    mean, scale = norm_stats(field, groups)
    return with_halo(norm_silu(field, mean, scale, groups), (("band", 1),), 1)


def taps_by_column(field):
    none = (0, 0)
    left = jnp.pad(field[:, :, :-1], (none, none, (1, 0)))
    right = jnp.pad(field[:, :, 1:], (none, none, (0, 1)))
    return jnp.concatenate([left, field, right], axis=1)


def wide_of(kernel):
    return kernel.shape[1] * kernel.shape[2]


def tap_weights(kernel):
    taps, cols, inner, outer = kernel.shape
    return jnp.transpose(kernel, (0, 3, 1, 2)).reshape(taps, outer, cols * inner)


def first_conv_kernel(x_ref, w_ref, d_ref, u_ref, s_ref, o_ref):
    row = pl.program_id(0)
    main = None
    low = None
    for tap in range(3):
        piece = x_ref[row + tap]
        dims = (((0,), (0,)), ((), ()))
        m = lax.dot_general(w_ref[tap], piece, dims, preferred_element_type=jnp.float32)
        l = lax.dot_general(d_ref[tap], piece, dims, preferred_element_type=jnp.float32)
        main = m if main is None else main + m
        low = l if low is None else low + l
    lifted = jnp.dot(u_ref[...], low.astype(jnp.bfloat16), preferred_element_type=jnp.float32)
    o_ref[0] = main + lifted + s_ref[...]


def second_conv_kernel(x_ref, w_ref, r_ref, o_ref):
    row = pl.program_id(0)
    total = None
    for tap in range(3):
        t = lax.dot_general(
            w_ref[tap], x_ref[row + tap], (((0,), (0,)), ((), ())), preferred_element_type=jnp.float32
        )
        total = t if total is None else total + t
    o_ref[0] = (r_ref[0].astype(jnp.float32) + total).astype(o_ref.dtype)


def first_conv(cols, weight, down, up_t, shift):
    rows, wide, width = cols.shape[0] - 2, cols.shape[1], cols.shape[2]
    out = weight.shape[2]
    rank = down.shape[2]
    flops = 2 * rows * width * wide * (out + rank) + 2 * rows * width * rank * out
    return pl.pallas_call(
        first_conv_kernel,
        grid=(rows,),
        in_specs=[
            pl.BlockSpec(cols.shape, lambda h: (0, 0, 0)),
            pl.BlockSpec(weight.shape, lambda h: (0, 0, 0)),
            pl.BlockSpec(down.shape, lambda h: (0, 0, 0)),
            pl.BlockSpec(up_t.shape, lambda h: (0, 0)),
            pl.BlockSpec(shift.shape, lambda h: (0, 0)),
        ],
        out_specs=pl.BlockSpec((1, out, width), lambda h: (h, 0, 0)),
        out_shape=jax.ShapeDtypeStruct((rows, out, width), jnp.float32),
        cost_estimate=pl.CostEstimate(
            flops=flops, transcendentals=0,
            bytes_accessed=cols.size * 2 + weight.size * 2 + down.size * 2 + rows * width * out * 4,
        ),
    )(cols, weight, down, up_t, shift)


def second_conv(cols, weight, residual):
    rows, wide, width = cols.shape[0] - 2, cols.shape[1], cols.shape[2]
    out = weight.shape[2]
    return pl.pallas_call(
        second_conv_kernel,
        grid=(rows,),
        in_specs=[
            pl.BlockSpec(cols.shape, lambda h: (0, 0, 0)),
            pl.BlockSpec(weight.shape, lambda h: (0, 0, 0)),
            pl.BlockSpec((1, out, width), lambda h: (h, 0, 0)),
        ],
        out_specs=pl.BlockSpec((1, out, width), lambda h: (h, 0, 0)),
        out_shape=jax.ShapeDtypeStruct((rows, out, width), residual.dtype),
        cost_estimate=pl.CostEstimate(
            flops=2 * rows * width * wide * out, transcendentals=0,
            bytes_accessed=cols.size * 2 + weight.size * 2 + rows * width * out * 4,
        ),
    )(cols, weight, residual)


def fetch_adapter(slots, down, up):
    bands, reqs = lax.axis_size("band"), lax.axis_size("req")
    flat = jnp.concatenate([down.reshape(-1), up.reshape(-1)])
    lanes, sublanes = 128, 16
    piece_rows = -(-flat.size // (bands * lanes * sublanes)) * sublanes
    flat = jnp.pad(flat, (0, bands * piece_rows * lanes - flat.size))
    pieces = flat.reshape(bands, piece_rows, lanes)
    by_band = lax.all_to_all(pieces, "band", 0, 0, tiled=True)
    wanted = jnp.take(by_band, slots // reqs, axis=0)
    by_req = lax.all_to_all(wanted, "req", 0, 0, tiled=True)
    own = lax.axis_index("req")
    mine = lax.dynamic_index_in_dim(by_req, slots[own] % reqs, 0, keepdims=False)
    whole = exchange(mine, "band").reshape(-1)
    down_size = down.size
    chosen_down = whole[:down_size].reshape(down.shape[1:])
    chosen_up = whole[down_size : down_size + up.size].reshape(up.shape[1:])
    return chosen_down, chosen_up


def shards(
    latents,
    request_time_embedding,
    request_adapter,
    adapter_stored_row,
    first_conv_weight,
    stored_down_weight,
    stored_up_weight,
    second_conv_weight,
    time_projection_weight,
):
    requests, rows, width, channels = latents.shape
    every_adapter = exchange(request_adapter[0, 0], "req")
    slots = jnp.take(adapter_stored_row, every_adapter, axis=0)
    chosen_down, chosen_up = fetch_adapter(slots, stored_down_weight, stored_up_weight)
    shift = jnp.dot(
        jax.nn.silu(request_time_embedding.astype(jnp.float32)).astype(jnp.bfloat16),
        time_projection_weight,
        preferred_element_type=jnp.float32,
    )
    field = jnp.swapaxes(latents, 2, 3)
    hidden = first_conv(
        taps_by_column(conv_input(field, G)[0]),
        first_conv_weight.reshape(3, wide_of(first_conv_weight), channels),
        chosen_down.reshape(3, wide_of(chosen_down), chosen_down.shape[-1]),
        chosen_up.T,
        shift.reshape(channels, 1),
    )[None]
    result = second_conv(
        taps_by_column(conv_input(hidden, G)[0]),
        second_conv_weight.reshape(3, wide_of(second_conv_weight), channels),
        field[0],
    )
    return jnp.swapaxes(result[None], 2, 3)


def solution(mesh):
    in_specs = (
        P("req", "band", None, None),
        P("req", None),
        P("req", None),
        P(),
        P(),
        P(("band", "req"), None, None, None, None),
        P(("band", "req"), None, None),
        P(),
        P(),
    )
    out_specs = P("req", "band", None, None)
    return jax.shard_map(shards, mesh=mesh, in_specs=in_specs, out_specs=out_specs, check_vma=False)
```

```python
import jax
import jax.numpy as jnp
from jax import lax
from jax.experimental import pallas as pl
from jax.sharding import PartitionSpec as P

G = 32


def with_halo(x, sides, width):
    for axis, dim in sides:
        count, length = (lax.axis_size(axis), x.shape[dim])
        up = [(i, (i + 1) % count) for i in range(count - 1)]
        down = [(j, i) for i, j in up]
        last = lax.slice_in_dim(x, length - width, length, axis=dim)
        initial = lax.slice_in_dim(x, 0, width, axis=dim)
        before = lax.ppermute(last, axis, up)
        after = lax.ppermute(initial, axis, down)
        x = jnp.concatenate([before, x, after], axis=dim)
    return x


def exchange(value, axis):
    count = lax.axis_size(axis)
    spread = jnp.broadcast_to(value[None], (count,) + value.shape)
    return lax.all_to_all(spread, axis, 0, 0, tiled=True)


def local_stats(field, groups):
    field = field.astype(jnp.float32)
    requests, rows, channels, width = field.shape
    grouped = field.reshape(requests, rows, groups, channels // groups, width)
    count = rows * width * (channels // groups)
    local_mean = jnp.sum(grouped, axis=(1, 3, 4)) / count
    deviation = grouped - local_mean[:, None, :, None, None]
    local_m2 = jnp.sum(deviation * deviation, axis=(1, 3, 4))
    return jnp.stack([local_mean, local_m2]), count


def combine_stats(stats, count):
    means, m2s = stats[:, 0], stats[:, 1]
    bands = means.shape[0]
    mean = jnp.sum(means, axis=0) / bands
    gap = means - mean[None]
    m2 = jnp.sum(m2s, axis=0) + count * jnp.sum(gap * gap, axis=0)
    spread = m2 / (count * bands)
    return mean, lax.rsqrt(spread + 1e-05)


def norm_stats(field, groups):
    stats, count = local_stats(field, groups)
    return combine_stats(exchange(stats, "band"), count)


def norm_silu(field, mean, scale, groups):
    field = field.astype(jnp.float32)
    requests, rows, channels, width = field.shape
    grouped = field.reshape(requests, rows, groups, channels // groups, width)
    normed = (grouped - mean[:, None, :, None, None]) * scale[:, None, :, None, None]
    return jax.nn.silu(normed.reshape(field.shape)).astype(jnp.bfloat16)


def conv_input(field, groups, norm=None):
    mean, scale = norm_stats(field, groups) if norm is None else norm
    return with_halo(norm_silu(field, mean, scale, groups), (("band", 1),), 1)


def taps_by_column(field):
    none = (0, 0)
    left = jnp.pad(field[:, :, :-1], (none, none, (1, 0)))
    right = jnp.pad(field[:, :, 1:], (none, none, (0, 1)))
    return jnp.concatenate([left, field, right], axis=1)


def wide_of(kernel):
    return kernel.shape[1] * kernel.shape[2]


def tap_weights(kernel):
    taps, cols, inner, outer = kernel.shape
    return jnp.transpose(kernel, (0, 3, 1, 2)).reshape(taps, outer, cols * inner)


def first_conv_kernel(x_ref, w_ref, d_ref, u_ref, s_ref, o_ref):
    row = pl.program_id(0)
    main = None
    low = None
    for tap in range(3):
        piece = x_ref[row + tap]
        dims = (((0,), (0,)), ((), ()))
        m = lax.dot_general(w_ref[tap], piece, dims, preferred_element_type=jnp.float32)
        l = lax.dot_general(d_ref[tap], piece, dims, preferred_element_type=jnp.float32)
        main = m if main is None else main + m
        low = l if low is None else low + l
    lifted = jnp.dot(u_ref[...], low.astype(jnp.bfloat16), preferred_element_type=jnp.float32)
    o_ref[0] = main + lifted + s_ref[...]


def second_conv_kernel(x_ref, w_ref, r_ref, o_ref):
    row = pl.program_id(0)
    total = None
    for tap in range(3):
        t = lax.dot_general(
            w_ref[tap], x_ref[row + tap], (((0,), (0,)), ((), ())), preferred_element_type=jnp.float32
        )
        total = t if total is None else total + t
    o_ref[0] = (r_ref[0].astype(jnp.float32) + total).astype(o_ref.dtype)


def first_conv(cols, weight, down, up_t, shift):
    rows, wide, width = cols.shape[0] - 2, cols.shape[1], cols.shape[2]
    out = weight.shape[2]
    rank = down.shape[2]
    flops = 2 * rows * width * wide * (out + rank) + 2 * rows * width * rank * out
    return pl.pallas_call(
        first_conv_kernel,
        grid=(rows,),
        in_specs=[
            pl.BlockSpec(cols.shape, lambda h: (0, 0, 0)),
            pl.BlockSpec(weight.shape, lambda h: (0, 0, 0)),
            pl.BlockSpec(down.shape, lambda h: (0, 0, 0)),
            pl.BlockSpec(up_t.shape, lambda h: (0, 0)),
            pl.BlockSpec(shift.shape, lambda h: (0, 0)),
        ],
        out_specs=pl.BlockSpec((1, out, width), lambda h: (h, 0, 0)),
        out_shape=jax.ShapeDtypeStruct((rows, out, width), jnp.float32),
        cost_estimate=pl.CostEstimate(
            flops=flops, transcendentals=0,
            bytes_accessed=cols.size * 2 + weight.size * 2 + down.size * 2 + rows * width * out * 4,
        ),
    )(cols, weight, down, up_t, shift)


def second_conv(cols, weight, residual):
    rows, wide, width = cols.shape[0] - 2, cols.shape[1], cols.shape[2]
    out = weight.shape[2]
    return pl.pallas_call(
        second_conv_kernel,
        grid=(rows,),
        in_specs=[
            pl.BlockSpec(cols.shape, lambda h: (0, 0, 0)),
            pl.BlockSpec(weight.shape, lambda h: (0, 0, 0)),
            pl.BlockSpec((1, out, width), lambda h: (h, 0, 0)),
        ],
        out_specs=pl.BlockSpec((1, out, width), lambda h: (h, 0, 0)),
        out_shape=jax.ShapeDtypeStruct((rows, out, width), residual.dtype),
        cost_estimate=pl.CostEstimate(
            flops=2 * rows * width * wide * out, transcendentals=0,
            bytes_accessed=cols.size * 2 + weight.size * 2 + rows * width * out * 4,
        ),
    )(cols, weight, residual)


def fetch_adapter(slots, down, up, extra):
    bands, reqs = lax.axis_size("band"), lax.axis_size("req")
    flat = jnp.concatenate([down.reshape(-1), up.reshape(-1)])
    lanes, sublanes = 128, 16
    piece_rows = -(-flat.size // (bands * lanes * sublanes)) * sublanes
    flat = jnp.pad(flat, (0, bands * piece_rows * lanes - flat.size))
    pieces = flat.reshape(bands, piece_rows, lanes).astype(jnp.float32)
    extra_flat = extra.reshape(-1)
    extra_rows = -(-extra_flat.size // (lanes * 8)) * 8
    extra_block = jnp.pad(extra_flat, (0, extra_rows * lanes - extra_flat.size)).reshape(extra_rows, lanes)
    sent = jnp.concatenate([pieces, jnp.broadcast_to(extra_block[None], (bands, extra_rows, lanes))], axis=1)
    received = lax.all_to_all(sent, "band", 0, 0, tiled=True)
    by_band = received[:, :piece_rows].astype(jnp.bfloat16)
    extras = received[:, piece_rows:].reshape(bands, -1)[:, : extra_flat.size].reshape((bands,) + extra.shape)
    wanted = jnp.take(by_band, slots // reqs, axis=0)
    by_req = lax.all_to_all(wanted, "req", 0, 0, tiled=True)
    own = lax.axis_index("req")
    mine = lax.dynamic_index_in_dim(by_req, slots[own] % reqs, 0, keepdims=False)
    whole = exchange(mine, "band").reshape(-1)
    down_size = down.size
    chosen_down = whole[:down_size].reshape(down.shape[1:])
    chosen_up = whole[down_size : down_size + up.size].reshape(up.shape[1:])
    return chosen_down, chosen_up, extras


def shards(
    latents,
    request_time_embedding,
    request_adapter,
    adapter_stored_row,
    first_conv_weight,
    stored_down_weight,
    stored_up_weight,
    second_conv_weight,
    time_projection_weight,
):
    requests, rows, width, channels = latents.shape
    every_adapter = exchange(request_adapter[0, 0], "req")
    slots = jnp.take(adapter_stored_row, every_adapter, axis=0)
    field = jnp.swapaxes(latents, 2, 3)
    first_stats, first_count = local_stats(field, G)
    chosen_down, chosen_up, every_stats = fetch_adapter(
        slots, stored_down_weight, stored_up_weight, first_stats
    )
    shift = jnp.dot(
        jax.nn.silu(request_time_embedding.astype(jnp.float32)).astype(jnp.bfloat16),
        time_projection_weight,
        preferred_element_type=jnp.float32,
    )
    hidden = first_conv(
        taps_by_column(conv_input(field, G, combine_stats(every_stats, first_count))[0]),
        first_conv_weight.reshape(3, wide_of(first_conv_weight), channels),
        chosen_down.reshape(3, wide_of(chosen_down), chosen_down.shape[-1]),
        chosen_up.T,
        shift.reshape(channels, 1),
    )[None]
    result = second_conv(
        taps_by_column(conv_input(hidden, G)[0]),
        second_conv_weight.reshape(3, wide_of(second_conv_weight), channels),
        field[0],
    )
    return jnp.swapaxes(result[None], 2, 3)


def solution(mesh):
    in_specs = (
        P("req", "band", None, None),
        P("req", None),
        P("req", None),
        P(),
        P(),
        P(("band", "req"), None, None, None, None),
        P(("band", "req"), None, None),
        P(),
        P(),
    )
    out_specs = P("req", "band", None, None)
    return jax.shard_map(shards, mesh=mesh, in_specs=in_specs, out_specs=out_specs, check_vma=False)
```

```python
import jax
import jax.numpy as jnp
from jax import lax
from jax.experimental import pallas as pl
from jax.sharding import PartitionSpec as P

G = 32


def with_halo(x, sides, width):
    for axis, dim in sides:
        count, length = (lax.axis_size(axis), x.shape[dim])
        up = [(i, (i + 1) % count) for i in range(count - 1)]
        down = [(j, i) for i, j in up]
        last = lax.slice_in_dim(x, length - width, length, axis=dim)
        initial = lax.slice_in_dim(x, 0, width, axis=dim)
        before = lax.ppermute(last, axis, up)
        after = lax.ppermute(initial, axis, down)
        x = jnp.concatenate([before, x, after], axis=dim)
    return x


def exchange(value, axis):
    count = lax.axis_size(axis)
    spread = jnp.broadcast_to(value[None], (count,) + value.shape)
    return lax.all_to_all(spread, axis, 0, 0, tiled=True)


def norm_stats(field, groups):
    field = field.astype(jnp.float32)
    requests, rows, channels, width = field.shape
    grouped = field.reshape(requests, rows, groups, channels // groups, width)
    count = rows * width * (channels // groups)
    local_mean = jnp.sum(grouped, axis=(1, 3, 4)) / count
    deviation = grouped - local_mean[:, None, :, None, None]
    local_m2 = jnp.sum(deviation * deviation, axis=(1, 3, 4))
    stats = exchange(jnp.stack([local_mean, local_m2]), "band")
    means, m2s = stats[:, 0], stats[:, 1]
    bands = means.shape[0]
    mean = jnp.sum(means, axis=0) / bands
    gap = means - mean[None]
    m2 = jnp.sum(m2s, axis=0) + count * jnp.sum(gap * gap, axis=0)
    spread = m2 / (count * bands)
    return mean, lax.rsqrt(spread + 1e-05)


def norm_silu(field, mean, scale, groups):
    field = field.astype(jnp.float32)
    requests, rows, channels, width = field.shape
    grouped = field.reshape(requests, rows, groups, channels // groups, width)
    normed = (grouped - mean[:, None, :, None, None]) * scale[:, None, :, None, None]
    return jax.nn.silu(normed.reshape(field.shape)).astype(jnp.bfloat16)


def conv_input(field, groups):
    mean, scale = norm_stats(field, groups)
    return with_halo(norm_silu(field, mean, scale, groups), (("band", 1),), 1)


def conv_input_early(field, groups):
    extended = with_halo(field, (("band", 1),), 1)
    mean, scale = norm_stats(field, groups)
    normed = norm_silu(extended, mean, scale, groups)
    band, bands = lax.axis_index("band"), lax.axis_size("band")
    row = lax.broadcasted_iota(jnp.int32, (1, normed.shape[1], 1, 1), 1)
    outside = ((row == 0) & (band == 0)) | ((row == normed.shape[1] - 1) & (band == bands - 1))
    return jnp.where(outside, jnp.zeros((), normed.dtype), normed)


def taps_by_column(field):
    none = (0, 0)
    left = jnp.pad(field[:, :, :-1], (none, none, (1, 0)))
    right = jnp.pad(field[:, :, 1:], (none, none, (0, 1)))
    return jnp.concatenate([left, field, right], axis=1)


def wide_of(kernel):
    return kernel.shape[1] * kernel.shape[2]


def tap_weights(kernel):
    taps, cols, inner, outer = kernel.shape
    return jnp.transpose(kernel, (0, 3, 1, 2)).reshape(taps, outer, cols * inner)


def first_conv_kernel(x_ref, w_ref, d_ref, u_ref, s_ref, o_ref):
    row = pl.program_id(0)
    main = None
    low = None
    for tap in range(3):
        piece = x_ref[row + tap]
        dims = (((0,), (0,)), ((), ()))
        m = lax.dot_general(w_ref[tap], piece, dims, preferred_element_type=jnp.float32)
        l = lax.dot_general(d_ref[tap], piece, dims, preferred_element_type=jnp.float32)
        main = m if main is None else main + m
        low = l if low is None else low + l
    lifted = jnp.dot(u_ref[...], low.astype(jnp.bfloat16), preferred_element_type=jnp.float32)
    o_ref[0] = main + lifted + s_ref[...]


def second_conv_kernel(x_ref, w_ref, r_ref, o_ref):
    row = pl.program_id(0)
    total = None
    for tap in range(3):
        t = lax.dot_general(
            w_ref[tap], x_ref[row + tap], (((0,), (0,)), ((), ())), preferred_element_type=jnp.float32
        )
        total = t if total is None else total + t
    o_ref[0] = (r_ref[0].astype(jnp.float32) + total).astype(o_ref.dtype)


def first_conv(cols, weight, down, up_t, shift):
    rows, wide, width = cols.shape[0] - 2, cols.shape[1], cols.shape[2]
    out = weight.shape[2]
    rank = down.shape[2]
    flops = 2 * rows * width * wide * (out + rank) + 2 * rows * width * rank * out
    return pl.pallas_call(
        first_conv_kernel,
        grid=(rows,),
        in_specs=[
            pl.BlockSpec(cols.shape, lambda h: (0, 0, 0)),
            pl.BlockSpec(weight.shape, lambda h: (0, 0, 0)),
            pl.BlockSpec(down.shape, lambda h: (0, 0, 0)),
            pl.BlockSpec(up_t.shape, lambda h: (0, 0)),
            pl.BlockSpec(shift.shape, lambda h: (0, 0)),
        ],
        out_specs=pl.BlockSpec((1, out, width), lambda h: (h, 0, 0)),
        out_shape=jax.ShapeDtypeStruct((rows, out, width), jnp.float32),
        cost_estimate=pl.CostEstimate(
            flops=flops, transcendentals=0,
            bytes_accessed=cols.size * 2 + weight.size * 2 + down.size * 2 + rows * width * out * 4,
        ),
    )(cols, weight, down, up_t, shift)


def second_conv(cols, weight, residual):
    rows, wide, width = cols.shape[0] - 2, cols.shape[1], cols.shape[2]
    out = weight.shape[2]
    return pl.pallas_call(
        second_conv_kernel,
        grid=(rows,),
        in_specs=[
            pl.BlockSpec(cols.shape, lambda h: (0, 0, 0)),
            pl.BlockSpec(weight.shape, lambda h: (0, 0, 0)),
            pl.BlockSpec((1, out, width), lambda h: (h, 0, 0)),
        ],
        out_specs=pl.BlockSpec((1, out, width), lambda h: (h, 0, 0)),
        out_shape=jax.ShapeDtypeStruct((rows, out, width), residual.dtype),
        cost_estimate=pl.CostEstimate(
            flops=2 * rows * width * wide * out, transcendentals=0,
            bytes_accessed=cols.size * 2 + weight.size * 2 + rows * width * out * 4,
        ),
    )(cols, weight, residual)


def fetch_adapter(slots, down, up):
    bands, reqs = lax.axis_size("band"), lax.axis_size("req")
    flat = jnp.concatenate([down.reshape(-1), up.reshape(-1)])
    lanes, sublanes = 128, 16
    piece_rows = -(-flat.size // (bands * lanes * sublanes)) * sublanes
    flat = jnp.pad(flat, (0, bands * piece_rows * lanes - flat.size))
    pieces = flat.reshape(bands, piece_rows, lanes)
    by_band = lax.all_to_all(pieces, "band", 0, 0, tiled=True)
    wanted = jnp.take(by_band, slots // reqs, axis=0)
    by_req = lax.all_to_all(wanted, "req", 0, 0, tiled=True)
    own = lax.axis_index("req")
    mine = lax.dynamic_index_in_dim(by_req, slots[own] % reqs, 0, keepdims=False)
    whole = exchange(mine, "band").reshape(-1)
    down_size = down.size
    chosen_down = whole[:down_size].reshape(down.shape[1:])
    chosen_up = whole[down_size : down_size + up.size].reshape(up.shape[1:])
    return chosen_down, chosen_up


def shards(
    latents,
    request_time_embedding,
    request_adapter,
    adapter_stored_row,
    first_conv_weight,
    stored_down_weight,
    stored_up_weight,
    second_conv_weight,
    time_projection_weight,
):
    requests, rows, width, channels = latents.shape
    every_adapter = exchange(request_adapter[0, 0], "req")
    slots = jnp.take(adapter_stored_row, every_adapter, axis=0)
    chosen_down, chosen_up = fetch_adapter(slots, stored_down_weight, stored_up_weight)
    shift = jnp.dot(
        jax.nn.silu(request_time_embedding.astype(jnp.float32)).astype(jnp.bfloat16),
        time_projection_weight,
        preferred_element_type=jnp.float32,
    )
    field = jnp.swapaxes(latents, 2, 3)
    hidden = first_conv(
        taps_by_column(conv_input(field, G)[0]),
        first_conv_weight.reshape(3, wide_of(first_conv_weight), channels),
        chosen_down.reshape(3, wide_of(chosen_down), chosen_down.shape[-1]),
        chosen_up.T,
        shift.reshape(channels, 1),
    )[None]
    result = second_conv(
        taps_by_column(conv_input_early(hidden, G)[0]),
        second_conv_weight.reshape(3, wide_of(second_conv_weight), channels),
        field[0],
    )
    return jnp.swapaxes(result[None], 2, 3)


def solution(mesh):
    in_specs = (
        P("req", "band", None, None),
        P("req", None),
        P("req", None),
        P(),
        P(),
        P(("band", "req"), None, None, None, None),
        P(("band", "req"), None, None),
        P(),
        P(),
    )
    out_specs = P("req", "band", None, None)
    return jax.shard_map(shards, mesh=mesh, in_specs=in_specs, out_specs=out_specs, check_vma=False)
```

```python
import jax
import jax.numpy as jnp
from jax import lax
from jax.experimental import pallas as pl
from jax.sharding import PartitionSpec as P

G = 32


def with_halo(x, sides, width):
    for axis, dim in sides:
        count, length = (lax.axis_size(axis), x.shape[dim])
        up = [(i, (i + 1) % count) for i in range(count - 1)]
        down = [(j, i) for i, j in up]
        last = lax.slice_in_dim(x, length - width, length, axis=dim)
        initial = lax.slice_in_dim(x, 0, width, axis=dim)
        before = lax.ppermute(last, axis, up)
        after = lax.ppermute(initial, axis, down)
        x = jnp.concatenate([before, x, after], axis=dim)
    return x


def exchange(value, axis):
    count = lax.axis_size(axis)
    spread = jnp.broadcast_to(value[None], (count,) + value.shape)
    return lax.all_to_all(spread, axis, 0, 0, tiled=True)


def norm_stats(field, groups):
    field = field.astype(jnp.float32)
    requests, rows, channels, width = field.shape
    grouped = field.reshape(requests, rows, groups, channels // groups, width)
    count = rows * width * (channels // groups)
    local_mean = jnp.sum(grouped, axis=(1, 3, 4)) / count
    deviation = grouped - local_mean[:, None, :, None, None]
    local_m2 = jnp.sum(deviation * deviation, axis=(1, 3, 4))
    stats = exchange(jnp.stack([local_mean, local_m2]), "band")
    means, m2s = stats[:, 0], stats[:, 1]
    bands = means.shape[0]
    mean = jnp.sum(means, axis=0) / bands
    gap = means - mean[None]
    m2 = jnp.sum(m2s, axis=0) + count * jnp.sum(gap * gap, axis=0)
    spread = m2 / (count * bands)
    return mean, lax.rsqrt(spread + 1e-05)


def norm_silu(field, mean, scale, groups):
    field = field.astype(jnp.float32)
    requests, rows, channels, width = field.shape
    grouped = field.reshape(requests, rows, groups, channels // groups, width)
    normed = (grouped - mean[:, None, :, None, None]) * scale[:, None, :, None, None]
    return jax.nn.silu(normed.reshape(field.shape)).astype(jnp.bfloat16)


def conv_input(field, groups):
    mean, scale = norm_stats(field, groups)
    return with_halo(norm_silu(field, mean, scale, groups), (("band", 1),), 1)


def taps_by_column(field):
    none = (0, 0)
    left = jnp.pad(field[:, :, :-1], (none, none, (1, 0)))
    right = jnp.pad(field[:, :, 1:], (none, none, (0, 1)))
    return jnp.concatenate([left, field, right], axis=1)


def wide_of(kernel):
    return kernel.shape[1] * kernel.shape[2]


def tap_weights(kernel):
    taps, cols, inner, outer = kernel.shape
    return jnp.transpose(kernel, (0, 3, 1, 2)).reshape(taps, outer, cols * inner)


def first_conv_kernel(x_ref, w_ref, d_ref, u_ref, s_ref, o_ref):
    row = pl.program_id(0)
    main = None
    low = None
    for tap in range(3):
        piece = x_ref[row + tap]
        dims = (((0,), (0,)), ((), ()))
        m = lax.dot_general(w_ref[tap], piece, dims, preferred_element_type=jnp.float32)
        l = lax.dot_general(d_ref[tap], piece, dims, preferred_element_type=jnp.float32)
        main = m if main is None else main + m
        low = l if low is None else low + l
    lifted = lax.dot_general(
        u_ref[...], low.astype(jnp.bfloat16), dims, preferred_element_type=jnp.float32
    )
    o_ref[0] = main + lifted + s_ref[...]


def second_conv_kernel(x_ref, w_ref, r_ref, o_ref):
    row = pl.program_id(0)
    total = None
    for tap in range(3):
        t = lax.dot_general(
            w_ref[tap], x_ref[row + tap], (((0,), (0,)), ((), ())), preferred_element_type=jnp.float32
        )
        total = t if total is None else total + t
    o_ref[0] = (r_ref[0].astype(jnp.float32) + total).astype(o_ref.dtype)


def first_conv(cols, weight, down, up_t, shift):
    rows, wide, width = cols.shape[0] - 2, cols.shape[1], cols.shape[2]
    out = weight.shape[2]
    rank = down.shape[2]
    flops = 2 * rows * width * wide * (out + rank) + 2 * rows * width * rank * out
    return pl.pallas_call(
        first_conv_kernel,
        grid=(rows,),
        in_specs=[
            pl.BlockSpec(cols.shape, lambda h: (0, 0, 0)),
            pl.BlockSpec(weight.shape, lambda h: (0, 0, 0)),
            pl.BlockSpec(down.shape, lambda h: (0, 0, 0)),
            pl.BlockSpec(up_t.shape, lambda h: (0, 0)),
            pl.BlockSpec(shift.shape, lambda h: (0, 0)),
        ],
        out_specs=pl.BlockSpec((1, out, width), lambda h: (h, 0, 0)),
        out_shape=jax.ShapeDtypeStruct((rows, out, width), jnp.float32),
        cost_estimate=pl.CostEstimate(
            flops=flops, transcendentals=0,
            bytes_accessed=cols.size * 2 + weight.size * 2 + down.size * 2 + rows * width * out * 4,
        ),
    )(cols, weight, down, up_t, shift)


def second_conv(cols, weight, residual):
    rows, wide, width = cols.shape[0] - 2, cols.shape[1], cols.shape[2]
    out = weight.shape[2]
    return pl.pallas_call(
        second_conv_kernel,
        grid=(rows,),
        in_specs=[
            pl.BlockSpec(cols.shape, lambda h: (0, 0, 0)),
            pl.BlockSpec(weight.shape, lambda h: (0, 0, 0)),
            pl.BlockSpec((1, out, width), lambda h: (h, 0, 0)),
        ],
        out_specs=pl.BlockSpec((1, out, width), lambda h: (h, 0, 0)),
        out_shape=jax.ShapeDtypeStruct((rows, out, width), residual.dtype),
        cost_estimate=pl.CostEstimate(
            flops=2 * rows * width * wide * out, transcendentals=0,
            bytes_accessed=cols.size * 2 + weight.size * 2 + rows * width * out * 4,
        ),
    )(cols, weight, residual)


def fetch_adapter(slots, down, up):
    bands, reqs = lax.axis_size("band"), lax.axis_size("req")
    flat = jnp.concatenate([down.reshape(-1), up.reshape(-1)])
    lanes, sublanes = 128, 16
    piece_rows = -(-flat.size // (bands * lanes * sublanes)) * sublanes
    flat = jnp.pad(flat, (0, bands * piece_rows * lanes - flat.size))
    pieces = flat.reshape(bands, piece_rows, lanes)
    by_band = lax.all_to_all(pieces, "band", 0, 0, tiled=True)
    wanted = jnp.take(by_band, slots // reqs, axis=0)
    by_req = lax.all_to_all(wanted, "req", 0, 0, tiled=True)
    own = lax.axis_index("req")
    mine = lax.dynamic_index_in_dim(by_req, slots[own] % reqs, 0, keepdims=False)
    whole = exchange(mine, "band").reshape(-1)
    down_size = down.size
    chosen_down = whole[:down_size].reshape(down.shape[1:])
    chosen_up = whole[down_size : down_size + up.size].reshape(up.shape[1:])
    return chosen_down, chosen_up


def shards(
    latents,
    request_time_embedding,
    request_adapter,
    adapter_stored_row,
    first_conv_weight,
    stored_down_weight,
    stored_up_weight,
    second_conv_weight,
    time_projection_weight,
):
    requests, rows, width, channels = latents.shape
    every_adapter = exchange(request_adapter[0, 0], "req")
    slots = jnp.take(adapter_stored_row, every_adapter, axis=0)
    chosen_down, chosen_up = fetch_adapter(slots, stored_down_weight, stored_up_weight)
    shift = jnp.dot(
        jax.nn.silu(request_time_embedding.astype(jnp.float32)).astype(jnp.bfloat16),
        time_projection_weight,
        preferred_element_type=jnp.float32,
    )
    field = jnp.swapaxes(latents, 2, 3)
    hidden = first_conv(
        taps_by_column(conv_input(field, G)[0]),
        first_conv_weight.reshape(3, wide_of(first_conv_weight), channels),
        chosen_down.reshape(3, wide_of(chosen_down), chosen_down.shape[-1]),
        chosen_up,
        shift.reshape(channels, 1),
    )[None]
    result = second_conv(
        taps_by_column(conv_input(hidden, G)[0]),
        second_conv_weight.reshape(3, wide_of(second_conv_weight), channels),
        field[0],
    )
    return jnp.swapaxes(result[None], 2, 3)


def solution(mesh):
    in_specs = (
        P("req", "band", None, None),
        P("req", None),
        P("req", None),
        P(),
        P(),
        P(("band", "req"), None, None, None, None),
        P(("band", "req"), None, None),
        P(),
        P(),
    )
    out_specs = P("req", "band", None, None)
    return jax.shard_map(shards, mesh=mesh, in_specs=in_specs, out_specs=out_specs, check_vma=False)
```
